128 devices in a mesh: section: 4 (over x_hi, core), blk: 32 (over z, x_lo, y).
Axes of the slice: x: 4 (x_hi: 2, x_lo: 2; x = x_hi * 2 + x_lo), y: 4, z: 4, core: 2. Of those that a mesh axis runs over, the one named last changes fastest.
Arguments:
- prog_ids: int32 [5120, 256], P('blk'), may hold values from 0 to 383, as said below
- spec_ids: int32 [5120, 256], P('blk'), may hold values from 0 to 383
- prog_table: bfloat16 [384, 2048], replicated, may hold values from -6 to 6
- spec_table: bfloat16 [384, 2048], replicated, may hold values from -6 to 6
- layer_weights: bfloat16 [8192, 2048], P('section'), may hold values from -0.125 to 0.125
- gains: float32 [4, 2048], P('section'), may hold values from 0.5 to 1.5
- prog_proj: bfloat16 [2048, 768], replicated, may hold values from -0.125 to 0.125
- spec_proj: bfloat16 [2048, 768], replicated, may hold values from -0.125 to 0.125
Outputs:
- layer_grads: float32 [8192, 2048], P(('section', 'blk'))
The draws below stay inside these ranges and needn't reach their ends.
Inputs may be any that keep to these rules, and one draw needn't show every extreme that they name: `prog_ids`: each program in the second half of the batch repeats, at most of its positions, the bytes of the program 5120/2 rows earlier; each program in an odd-numbered block of 160 rows repeats nearly all bytes of the program 160 rows earlier; each specification repeats most bytes of its own program.
All inputs are finite; a program needn't handle non-finite values.
Results may differ from the reference program's by a relative error of at most 0.0065.
Values may be sent and summed in bfloat16 or wider, within the bound.
No kernel may reach another device: no remote copies, remote signals or barrier semaphores. Data moves between devices by JAX's collectives and lax.ppermute only.
A program may use at most 128 MiB of HBM per device.

```python
import jax
import jax.numpy as jnp
from jax import lax

D = 2048
E = 768
V = 384
L = 256
ROWS = 160
BATCH = 5120
N_SECTION = 4


def paired_ids(key):
    keys = jax.random.split(jax.random.fold_in(key, 4711), 6)
    half = BATCH // 2
    first = jax.random.randint(keys[0], (half, L), 0, V, dtype=jnp.int32)
    fresh = jax.random.randint(keys[1], (half, L), 0, V, dtype=jnp.int32)
    repeat = jax.random.randint(keys[2], (half, L), 0, 20, dtype=jnp.int32) < 17
    second = jnp.where(repeat, first, fresh)
    programs = jnp.concatenate([first, second], axis=0)
    pairs = BATCH // (2 * ROWS)
    grouped = programs.reshape(pairs, 2, ROWS, L)
    copy = jax.random.randint(keys[5], (pairs, ROWS, L), 0, 20, dtype=jnp.int32) < 19
    odd_blocks = jnp.where(copy, grouped[:, 0], grouped[:, 1])
    programs = jnp.stack([grouped[:, 0], odd_blocks], axis=1).reshape(BATCH, L)
    other = jax.random.randint(keys[3], (BATCH, L), 0, V, dtype=jnp.int32)
    keep = jax.random.randint(keys[4], (BATCH, L), 0, 10, dtype=jnp.int32) < 9
    specs = jnp.where(keep, programs, other)
    return (programs, specs)


def draw_prog_ids(key, part):
    return paired_ids(key)[0]


def draw_spec_ids(key, part):
    return paired_ids(key)[1]


def levels(own_key, shape, cuts, smallest, top_value):
    def one(axis_at, shards_of):
        heights = jax.random.uniform(jax.random.fold_in(jax.random.fold_in(own_key, 6), axis_at), (shards_of,), jnp.float32, smallest / len(cuts), top_value / len(cuts))
        return jnp.repeat(jnp.exp(heights), shape[axis_at] // shards_of).reshape((-1,) + (1,) * (len(shape) - axis_at - 1))

    level = one(*cuts[0])
    for cut in cuts[1:]:
        level = level * one(*cut)
    return level


def bell_draw(own_key, shape, scale, limit, pieces=(), kind=jnp.bfloat16):
    values = jax.random.normal(own_key, shape, jnp.float32) * scale
    if len(pieces) > 0:
        values = levels(own_key, shape, pieces, -0.22, 0.18) * values
    return jnp.clip(values, min=-limit, max=limit).astype(kind)


def setup_inputs(seed: int = 0) -> dict:
    seeds = jax.random.split(jax.random.key(seed), 9)
    prog_ids = draw_prog_ids(jax.random.fold_in(seeds[8], 71), 0)
    spec_ids = draw_spec_ids(jax.random.fold_in(seeds[8], 71), 0)
    prog_table = bell_draw(seeds[2], (V, D), 1.0, 6.0)
    spec_table = bell_draw(seeds[3], (V, D), 1.0, 6.0)
    layer_weights = bell_draw(seeds[4], (N_SECTION * D, D), D ** -0.5, 0.125, ((0, 4),))
    gains = jnp.clip(1.0 + 0.1 * jax.random.normal(seeds[5], (N_SECTION, D), jnp.float32), 0.5, 1.5)
    prog_proj = bell_draw(seeds[6], (D, E), D ** -0.5, 0.125)
    spec_proj = bell_draw(seeds[7], (D, E), D ** -0.5, 0.125)
    return dict(prog_ids=prog_ids, spec_ids=spec_ids, prog_table=prog_table, spec_table=spec_table, layer_weights=layer_weights, gains=gains, prog_proj=prog_proj, spec_proj=spec_proj)


logit_scale = 30.0
norm_eps = 1e-06

def bag_rows(token_ids, table):
    vocab_iota = jnp.arange(table.shape[0], dtype=jnp.int32)
    blocks = token_ids.reshape(-1, ROWS, token_ids.shape[1])

    def one_block(block):
        counts = lax.optimization_barrier(jnp.sum((block[:, :, None] == vocab_iota[None, None, :]).astype(jnp.float32), axis=1)).astype(jnp.bfloat16)
        return (jnp.dot(counts, table, preferred_element_type=jnp.float32) * (1.0 / L)).astype(jnp.bfloat16)
    return lax.map(one_block, blocks).reshape(token_ids.shape[0], table.shape[1])

def layer_parts(hidden, weight, gain):
    wide = hidden.astype(jnp.float32)
    inverse = lax.rsqrt(lax.optimization_barrier(jnp.mean(wide * wide, axis=1, keepdims=True)) + norm_eps)
    normed = wide * inverse
    scaled = (normed * gain).astype(jnp.bfloat16)
    mixed = jnp.dot(scaled, weight, preferred_element_type=jnp.float32)
    return (wide, inverse, normed, scaled, mixed)

def layer_forward(hidden, weight, gain):
    wide, inverse, normed, scaled, mixed = layer_parts(hidden, weight, gain)
    return (wide + mixed * jax.nn.sigmoid(mixed)).astype(jnp.bfloat16)

def layer_backward(hidden, upstream, weight, gain):
    wide, inverse, normed, scaled, mixed = layer_parts(hidden, weight, gain)
    sigma = jax.nn.sigmoid(mixed)
    up_wide = upstream.astype(jnp.float32)
    dmixed = (up_wide * sigma * (1.0 + mixed * (1.0 - sigma))).astype(jnp.bfloat16)
    wgrad = jnp.dot(scaled.T, dmixed, preferred_element_type=jnp.float32)
    dnormed = jnp.dot(dmixed, weight.T, preferred_element_type=jnp.float32) * gain
    dhidden = (up_wide + inverse * (dnormed - normed * lax.optimization_barrier(jnp.mean(dnormed * normed, axis=1, keepdims=True)))).astype(jnp.bfloat16)
    return (dhidden, wgrad)

def embed_rows(hidden, proj):
    emb = jnp.dot(hidden, proj, preferred_element_type=jnp.float32)
    inverse = lax.rsqrt(lax.optimization_barrier(jnp.sum(emb * emb, axis=1, keepdims=True)) + norm_eps)
    unit = emb * inverse
    return (unit, inverse, unit.astype(jnp.bfloat16))

def embed_back(dkey, unit, inverse):
    return (inverse * (dkey - unit * lax.optimization_barrier(jnp.sum(unit * dkey, axis=1, keepdims=True)))).astype(jnp.bfloat16)

def reference(prog_ids, spec_ids, prog_table, spec_table, layer_weights, gains, prog_proj, spec_proj):
    width = prog_table.shape[1]
    weights = [layer_weights[k * width:(k + 1) * width] for k in range(4)]
    prog_bag = bag_rows(prog_ids, prog_table)
    spec_bag = bag_rows(spec_ids, spec_table)
    prog_1 = layer_forward(prog_bag, weights[0], gains[0])
    prog_2 = layer_forward(prog_1, weights[1], gains[1])
    prog_3 = layer_forward(prog_2, weights[2], gains[2])
    spec_top = layer_forward(spec_bag, weights[3], gains[3])
    prog_unit, prog_inv, prog_key = embed_rows(prog_3, prog_proj)
    spec_unit, spec_inv, spec_key = embed_rows(spec_top, spec_proj)
    scores = logit_scale * jnp.dot(spec_key, prog_key.T, preferred_element_type=jnp.float32)
    row_max = lax.optimization_barrier(jnp.max(scores, axis=1, keepdims=True))
    lse = row_max + jnp.log(lax.optimization_barrier(jnp.sum(jnp.exp(scores - row_max), axis=1, keepdims=True)))
    probs = jnp.exp(scores - lse).astype(jnp.bfloat16)
    spec_dkey = logit_scale * (jnp.dot(probs, prog_key, preferred_element_type=jnp.float32) - prog_key.astype(jnp.float32))
    prog_dkey = logit_scale * (jnp.dot(probs.T, spec_key, preferred_element_type=jnp.float32) - spec_key.astype(jnp.float32))
    prog_demb = embed_back(prog_dkey, prog_unit, prog_inv)
    spec_demb = embed_back(spec_dkey, spec_unit, spec_inv)
    prog_d3 = jnp.dot(prog_demb, prog_proj.T, preferred_element_type=jnp.float32).astype(jnp.bfloat16)
    spec_dtop = jnp.dot(spec_demb, spec_proj.T, preferred_element_type=jnp.float32).astype(jnp.bfloat16)
    prog_d2, grad_two = layer_backward(prog_2, prog_d3, weights[2], gains[2])
    prog_d1, grad_one = layer_backward(prog_1, prog_d2, weights[1], gains[1])
    unused_zero, grad_zero = layer_backward(prog_bag, prog_d1, weights[0], gains[0])
    unused_spec, grad_three = layer_backward(spec_bag, spec_dtop, weights[3], gains[3])
    return jnp.concatenate([grad_zero, grad_one, grad_two, grad_three], axis=0)
```

```python
import jax
import jax.numpy as jnp
from jax import lax
from jax.sharding import PartitionSpec as P

L = 256
MICRO = 4


logit_scale = 30.0
norm_eps = 1e-06


def shift_pairs(axis, pairs):
    return lambda value: lax.ppermute(value, axis, pairs)


def gather_rows(value, axis):
    count = lax.axis_size(axis)
    spread = jnp.broadcast_to(value[None], (count,) + value.shape)
    got = lax.all_to_all(spread, axis, 0, 0, tiled=True)
    return got.reshape((count * value.shape[0],) + value.shape[1:])


def layer_parts(hidden, weight, gain):
    wide = hidden.astype(jnp.float32)
    inverse = lax.rsqrt(jnp.mean(wide * wide, axis=1, keepdims=True) + norm_eps)
    normed = wide * inverse
    scaled = (normed * gain).astype(jnp.bfloat16)
    mixed = jnp.dot(scaled, weight, preferred_element_type=jnp.float32)
    return (wide, inverse, normed, scaled, mixed)


def layer_forward(hidden, weight, gain):
    wide, inverse, normed, scaled, mixed = layer_parts(hidden, weight, gain)
    return (wide + mixed * jax.nn.sigmoid(mixed)).astype(jnp.bfloat16)


def layer_backward(hidden, upstream, weight, gain):
    wide, inverse, normed, scaled, mixed = layer_parts(hidden, weight, gain)
    sigma = jax.nn.sigmoid(mixed)
    up_wide = upstream.astype(jnp.float32)
    dmixed = (up_wide * sigma * (1.0 + mixed * (1.0 - sigma))).astype(jnp.bfloat16)
    dnormed = (
        lax.dot_general(
            dmixed, weight, (((1,), (1,)), ((), ())), preferred_element_type=jnp.float32
        )
        * gain
    )
    dhidden = (
        up_wide + inverse * (dnormed - normed * jnp.mean(dnormed * normed, axis=1, keepdims=True))
    ).astype(jnp.bfloat16)
    return (dhidden, scaled, dmixed)


def embed_rows(hidden, proj):
    emb = jnp.dot(hidden, proj, preferred_element_type=jnp.float32)
    inverse = lax.rsqrt(jnp.sum(emb * emb, axis=1, keepdims=True) + norm_eps)
    unit = emb * inverse
    return (unit, inverse, unit.astype(jnp.bfloat16))


def embed_back(dkey, unit, inverse, proj):
    demb = (inverse * (dkey - unit * jnp.sum(unit * dkey, axis=1, keepdims=True))).astype(
        jnp.bfloat16
    )
    return lax.dot_general(
        demb, proj, (((1,), (1,)), ((), ())), preferred_element_type=jnp.float32
    ).astype(jnp.bfloat16)


def keep_where(buffer, value, index, valid):
    previous = lax.dynamic_index_in_dim(buffer, index, 0, keepdims=False)
    return lax.dynamic_update_index_in_dim(buffer, jnp.where(valid, value, previous), index, 0)


def local(prog_ids, spec_ids, prog_table, spec_table, layer_weights, gains, prog_proj, spec_proj):
    section_index = lax.axis_index("section")
    last_section = lax.axis_size("section") - 1
    top_section = last_section - 1
    spec_section = section_index == last_section
    token_ids = jnp.where(spec_section, spec_ids, prog_ids)
    table = jnp.where(spec_section, spec_table, prog_table)
    vocab_iota = jnp.arange(table.shape[0], dtype=jnp.int32)
    counts = jnp.sum(
        (token_ids[:, :, None] == vocab_iota[None, None, :]).astype(jnp.float32), axis=1
    ).astype(jnp.bfloat16)
    sample_rows = prog_ids.shape[0]
    micro_rows = sample_rows // MICRO
    width = layer_weights.shape[1]
    first_inputs = (jnp.dot(counts, table, preferred_element_type=jnp.float32) * (1.0 / L)).astype(
        jnp.bfloat16
    )
    first_inputs = first_inputs.reshape(MICRO, micro_rows, width)
    gain = gains[0]
    blank = jnp.zeros((MICRO, micro_rows, width), jnp.bfloat16)
    saved_inputs = blank
    tops = blank
    received = jnp.zeros((micro_rows, width), jnp.bfloat16)
    forward_offset = jnp.where(spec_section, 0, section_index)
    takes_bag = spec_section | (section_index == 0)
    to_next = shift_pairs("section", [(s, s + 1) for s in range(top_section)])
    for moment in range(MICRO + top_section):
        micro_index = moment - forward_offset
        in_range = (micro_index >= 0) & (micro_index < MICRO)
        clipped = jnp.clip(micro_index, 0, MICRO - 1)
        from_bag = lax.dynamic_index_in_dim(first_inputs, clipped, 0, keepdims=False)
        current = jnp.where(takes_bag, from_bag, received)
        saved_inputs = keep_where(saved_inputs, current, clipped, in_range)
        output = layer_forward(current, layer_weights, gain)
        tops = keep_where(tops, output, clipped, in_range)
        if moment + 1 < MICRO + top_section:
            received = to_next(output)
    proj = jnp.where(spec_section, spec_proj, prog_proj)
    unit, inverse, key = embed_rows(tops.reshape(sample_rows, width), proj)
    swap = shift_pairs("section", [(top_section, last_section), (last_section, top_section)])
    partner_key = swap(key)
    others = gather_rows(partner_key, "blk")
    scores = logit_scale * lax.dot_general(
        key, others, (((1,), (1,)), ((), ())), preferred_element_type=jnp.float32
    )
    row_max = jnp.max(scores, axis=1, keepdims=True)
    lse = row_max + jnp.log(jnp.sum(jnp.exp(scores - row_max), axis=1, keepdims=True))
    lse_down = shift_pairs("section", [(last_section, top_section)])(lse)
    lse_all = gather_rows(lse_down, "blk").reshape(1, -1)
    shift = jnp.where(spec_section, lse, lse_all)
    probs = jnp.exp(scores - shift).astype(jnp.bfloat16)
    dkey = logit_scale * (
        jnp.dot(probs, others, preferred_element_type=jnp.float32)
        - partner_key.astype(jnp.float32)
    )
    top_grad = embed_back(dkey, unit, inverse, proj).reshape(MICRO, micro_rows, width)
    saved_scaled = blank
    saved_dmixed = blank
    starts_grad = section_index >= top_section
    backward_offset = jnp.where(starts_grad, 0, top_section - section_index)
    to_previous = shift_pairs("section", [(s, s - 1) for s in range(1, top_section + 1)])
    incoming = jnp.zeros((micro_rows, width), jnp.bfloat16)
    for moment in range(MICRO + top_section):
        if moment > 0:
            incoming = to_previous(dhidden)
        micro_index = moment - backward_offset
        in_range = (micro_index >= 0) & (micro_index < MICRO)
        clipped = jnp.clip(micro_index, 0, MICRO - 1)
        upstream = jnp.where(
            starts_grad, lax.dynamic_index_in_dim(top_grad, clipped, 0, keepdims=False), incoming
        )
        hidden = lax.dynamic_index_in_dim(saved_inputs, clipped, 0, keepdims=False)
        dhidden, scaled, dmixed = layer_backward(hidden, upstream, layer_weights, gain)
        saved_scaled = keep_where(saved_scaled, scaled, clipped, in_range)
        saved_dmixed = keep_where(saved_dmixed, dmixed, clipped, in_range)
    scaled_all = saved_scaled.reshape(sample_rows, width)
    dmixed_all = saved_dmixed.reshape(sample_rows, width)
    partial = lax.dot_general(
        scaled_all, dmixed_all, (((0,), (0,)), ((), ())), preferred_element_type=jnp.float32
    )
    count = lax.axis_size("blk")
    pieces = partial.astype(jnp.bfloat16).reshape(count, width // count, width)
    landed = lax.all_to_all(pieces, "blk", 0, 0, tiled=True)
    return jnp.sum(landed.astype(jnp.float32), axis=0)


def solution(mesh):
    return jax.shard_map(
        local,
        mesh=mesh,
        in_specs=(
            P("blk", None),
            P("blk", None),
            P(),
            P(),
            P("section", None),
            P("section", None),
            P(),
            P(),
        ),
        out_specs=P(("section", "blk"), None),
        check_vma=False,
    )
```

```python
import jax
import jax.numpy as jnp
from jax import lax
from jax.sharding import PartitionSpec as P

L = 256
MICRO = 1


logit_scale = 30.0
norm_eps = 1e-06


def shift_pairs(axis, pairs):
    return lambda value: lax.ppermute(value, axis, pairs)


def gather_rows(value, axis):
    count = lax.axis_size(axis)
    spread = jnp.broadcast_to(value[None], (count,) + value.shape)
    got = lax.all_to_all(spread, axis, 0, 0, tiled=True)
    return got.reshape((count * value.shape[0],) + value.shape[1:])


def layer_parts(hidden, weight, gain):
    wide = hidden.astype(jnp.float32)
    inverse = lax.rsqrt(jnp.mean(wide * wide, axis=1, keepdims=True) + norm_eps)
    normed = wide * inverse
    scaled = (normed * gain).astype(jnp.bfloat16)
    mixed = jnp.dot(scaled, weight, preferred_element_type=jnp.float32)
    return (wide, inverse, normed, scaled, mixed)


def layer_forward(hidden, weight, gain):
    wide, inverse, normed, scaled, mixed = layer_parts(hidden, weight, gain)
    return (wide + mixed * jax.nn.sigmoid(mixed)).astype(jnp.bfloat16)


def layer_backward(hidden, upstream, weight, gain):
    wide, inverse, normed, scaled, mixed = layer_parts(hidden, weight, gain)
    sigma = jax.nn.sigmoid(mixed)
    up_wide = upstream.astype(jnp.float32)
    dmixed = (up_wide * sigma * (1.0 + mixed * (1.0 - sigma))).astype(jnp.bfloat16)
    dnormed = (
        lax.dot_general(
            dmixed, weight, (((1,), (1,)), ((), ())), preferred_element_type=jnp.float32
        )
        * gain
    )
    dhidden = (
        up_wide + inverse * (dnormed - normed * jnp.mean(dnormed * normed, axis=1, keepdims=True))
    ).astype(jnp.bfloat16)
    return (dhidden, scaled, dmixed)


def embed_rows(hidden, proj):
    emb = jnp.dot(hidden, proj, preferred_element_type=jnp.float32)
    inverse = lax.rsqrt(jnp.sum(emb * emb, axis=1, keepdims=True) + norm_eps)
    unit = emb * inverse
    return (unit, inverse, unit.astype(jnp.bfloat16))


def embed_back(dkey, unit, inverse, proj):
    demb = (inverse * (dkey - unit * jnp.sum(unit * dkey, axis=1, keepdims=True))).astype(
        jnp.bfloat16
    )
    return lax.dot_general(
        demb, proj, (((1,), (1,)), ((), ())), preferred_element_type=jnp.float32
    ).astype(jnp.bfloat16)


def keep_where(buffer, value, index, valid):
    previous = lax.dynamic_index_in_dim(buffer, index, 0, keepdims=False)
    return lax.dynamic_update_index_in_dim(buffer, jnp.where(valid, value, previous), index, 0)


def local(prog_ids, spec_ids, prog_table, spec_table, layer_weights, gains, prog_proj, spec_proj):
    section_index = lax.axis_index("section")
    last_section = lax.axis_size("section") - 1
    top_section = last_section - 1
    spec_section = section_index == last_section
    token_ids = jnp.where(spec_section, spec_ids, prog_ids)
    table = jnp.where(spec_section, spec_table, prog_table)
    vocab_iota = jnp.arange(table.shape[0], dtype=jnp.int32)
    counts = jnp.sum(
        (token_ids[:, :, None] == vocab_iota[None, None, :]).astype(jnp.float32), axis=1
    ).astype(jnp.bfloat16)
    sample_rows = prog_ids.shape[0]
    micro_rows = sample_rows // MICRO
    width = layer_weights.shape[1]
    first_inputs = (jnp.dot(counts, table, preferred_element_type=jnp.float32) * (1.0 / L)).astype(
        jnp.bfloat16
    )
    first_inputs = first_inputs.reshape(MICRO, micro_rows, width)
    gain = gains[0]
    blank = jnp.zeros((MICRO, micro_rows, width), jnp.bfloat16)
    saved_inputs = blank
    tops = blank
    received = jnp.zeros((micro_rows, width), jnp.bfloat16)
    forward_offset = jnp.where(spec_section, 0, section_index)
    takes_bag = spec_section | (section_index == 0)
    to_next = shift_pairs("section", [(s, s + 1) for s in range(top_section)])
    for moment in range(MICRO + top_section):
        micro_index = moment - forward_offset
        in_range = (micro_index >= 0) & (micro_index < MICRO)
        clipped = jnp.clip(micro_index, 0, MICRO - 1)
        from_bag = lax.dynamic_index_in_dim(first_inputs, clipped, 0, keepdims=False)
        current = jnp.where(takes_bag, from_bag, received)
        saved_inputs = keep_where(saved_inputs, current, clipped, in_range)
        output = layer_forward(current, layer_weights, gain)
        tops = keep_where(tops, output, clipped, in_range)
        if moment + 1 < MICRO + top_section:
            received = to_next(output)
    proj = jnp.where(spec_section, spec_proj, prog_proj)
    unit, inverse, key = embed_rows(tops.reshape(sample_rows, width), proj)
    swap = shift_pairs("section", [(top_section, last_section), (last_section, top_section)])
    partner_key = swap(key)
    others = gather_rows(partner_key, "blk")
    scores = logit_scale * lax.dot_general(
        key, others, (((1,), (1,)), ((), ())), preferred_element_type=jnp.float32
    )
    row_max = jnp.max(scores, axis=1, keepdims=True)
    lse = row_max + jnp.log(jnp.sum(jnp.exp(scores - row_max), axis=1, keepdims=True))
    lse_down = shift_pairs("section", [(last_section, top_section)])(lse)
    lse_all = gather_rows(lse_down, "blk").reshape(1, -1)
    shift = jnp.where(spec_section, lse, lse_all)
    probs = jnp.exp(scores - shift).astype(jnp.bfloat16)
    dkey = logit_scale * (
        jnp.dot(probs, others, preferred_element_type=jnp.float32)
        - partner_key.astype(jnp.float32)
    )
    top_grad = embed_back(dkey, unit, inverse, proj).reshape(MICRO, micro_rows, width)
    saved_scaled = blank
    saved_dmixed = blank
    starts_grad = section_index >= top_section
    backward_offset = jnp.where(starts_grad, 0, top_section - section_index)
    to_previous = shift_pairs("section", [(s, s - 1) for s in range(1, top_section + 1)])
    incoming = jnp.zeros((micro_rows, width), jnp.bfloat16)
    for moment in range(MICRO + top_section):
        if moment > 0:
            incoming = to_previous(dhidden)
        micro_index = moment - backward_offset
        in_range = (micro_index >= 0) & (micro_index < MICRO)
        clipped = jnp.clip(micro_index, 0, MICRO - 1)
        upstream = jnp.where(
            starts_grad, lax.dynamic_index_in_dim(top_grad, clipped, 0, keepdims=False), incoming
        )
        hidden = lax.dynamic_index_in_dim(saved_inputs, clipped, 0, keepdims=False)
        dhidden, scaled, dmixed = layer_backward(hidden, upstream, layer_weights, gain)
        saved_scaled = keep_where(saved_scaled, scaled, clipped, in_range)
        saved_dmixed = keep_where(saved_dmixed, dmixed, clipped, in_range)
    scaled_all = saved_scaled.reshape(sample_rows, width)
    dmixed_all = saved_dmixed.reshape(sample_rows, width)
    partial = lax.dot_general(
        scaled_all, dmixed_all, (((0,), (0,)), ((), ())), preferred_element_type=jnp.float32
    )
    count = lax.axis_size("blk")
    pieces = partial.astype(jnp.bfloat16).reshape(count, width // count, width)
    landed = lax.all_to_all(pieces, "blk", 0, 0, tiled=True)
    return jnp.sum(landed.astype(jnp.float32), axis=0)


def solution(mesh):
    return jax.shard_map(
        local,
        mesh=mesh,
        in_specs=(
            P("blk", None),
            P("blk", None),
            P(),
            P(),
            P("section", None),
            P("section", None),
            P(),
            P(),
        ),
        out_specs=P(("section", "blk"), None),
        check_vma=False,
    )
```

```python
import jax
import jax.numpy as jnp
from jax import lax
from jax.sharding import PartitionSpec as P

L = 256
MICRO = 1


logit_scale = 30.0
norm_eps = 1e-06


def shift_pairs(axis, pairs):
    return lambda value: lax.ppermute(value, axis, pairs)


def gather_rows(value, axis):
    count = lax.axis_size(axis)
    spread = jnp.broadcast_to(value[None], (count,) + value.shape)
    got = lax.all_to_all(spread, axis, 0, 0, tiled=True)
    return got.reshape((count * value.shape[0],) + value.shape[1:])


def layer_parts(hidden, weight, gain):
    wide = hidden.astype(jnp.float32)
    inverse = lax.rsqrt(jnp.mean(wide * wide, axis=1, keepdims=True) + norm_eps)
    normed = wide * inverse
    scaled = (normed * gain).astype(jnp.bfloat16)
    mixed = jnp.dot(scaled, weight, preferred_element_type=jnp.float32)
    return (wide, inverse, normed, scaled, mixed)


def layer_forward(hidden, weight, gain):
    wide, inverse, normed, scaled, mixed = layer_parts(hidden, weight, gain)
    return (wide + mixed * jax.nn.sigmoid(mixed)).astype(jnp.bfloat16)


def layer_backward(hidden, upstream, weight, gain):
    wide, inverse, normed, scaled, mixed = layer_parts(hidden, weight, gain)
    sigma = jax.nn.sigmoid(mixed)
    up_wide = upstream.astype(jnp.float32)
    dmixed = (up_wide * sigma * (1.0 + mixed * (1.0 - sigma))).astype(jnp.bfloat16)
    dnormed = (
        lax.dot_general(
            dmixed, weight, (((1,), (1,)), ((), ())), preferred_element_type=jnp.float32
        )
        * gain
    )
    dhidden = (
        up_wide + inverse * (dnormed - normed * jnp.mean(dnormed * normed, axis=1, keepdims=True))
    ).astype(jnp.bfloat16)
    return (dhidden, scaled, dmixed)


def embed_rows(hidden, proj):
    emb = jnp.dot(hidden, proj, preferred_element_type=jnp.float32)
    inverse = lax.rsqrt(jnp.sum(emb * emb, axis=1, keepdims=True) + norm_eps)
    unit = emb * inverse
    return (unit, inverse, unit.astype(jnp.bfloat16))


def embed_back(dkey, unit, inverse, proj):
    demb = (inverse * (dkey - unit * jnp.sum(unit * dkey, axis=1, keepdims=True))).astype(
        jnp.bfloat16
    )
    return lax.dot_general(
        demb, proj, (((1,), (1,)), ((), ())), preferred_element_type=jnp.float32
    ).astype(jnp.bfloat16)


def keep_where(buffer, value, index, valid):
    previous = lax.dynamic_index_in_dim(buffer, index, 0, keepdims=False)
    return lax.dynamic_update_index_in_dim(buffer, jnp.where(valid, value, previous), index, 0)


def local(prog_ids, spec_ids, prog_table, spec_table, layer_weights, gains, prog_proj, spec_proj):
    section_index = lax.axis_index("section")
    last_section = lax.axis_size("section") - 1
    top_section = last_section - 1
    spec_section = section_index == last_section
    token_ids = jnp.where(spec_section, spec_ids, prog_ids)
    table = jnp.where(spec_section, spec_table, prog_table)
    vocab_iota = jnp.arange(table.shape[0], dtype=jnp.int32)
    counts = jnp.sum(
        (token_ids[:, :, None] == vocab_iota[None, None, :]).astype(jnp.float32), axis=1
    ).astype(jnp.bfloat16)
    sample_rows = prog_ids.shape[0]
    micro_rows = sample_rows // MICRO
    width = layer_weights.shape[1]
    first_inputs = (jnp.dot(counts, table, preferred_element_type=jnp.float32) * (1.0 / L)).astype(
        jnp.bfloat16
    )
    first_inputs = first_inputs.reshape(MICRO, micro_rows, width)
    gain = gains[0]
    blank = jnp.zeros((MICRO, micro_rows, width), jnp.bfloat16)
    saved_inputs = blank
    tops = blank
    received = jnp.zeros((micro_rows, width), jnp.bfloat16)
    forward_offset = jnp.where(spec_section, 0, section_index)
    takes_bag = spec_section | (section_index == 0)
    for moment in range(MICRO + top_section):
        micro_index = moment - forward_offset
        in_range = (micro_index >= 0) & (micro_index < MICRO)
        clipped = jnp.clip(micro_index, 0, MICRO - 1)
        from_bag = lax.dynamic_index_in_dim(first_inputs, clipped, 0, keepdims=False)
        current = jnp.where(takes_bag, from_bag, received)
        saved_inputs = keep_where(saved_inputs, current, clipped, in_range)
        output = layer_forward(current, layer_weights, gain)
        tops = keep_where(tops, output, clipped, in_range)
        senders = [s for s in range(top_section) if 0 <= moment - s < MICRO]
        if senders:
            received = shift_pairs("section", [(s, s + 1) for s in senders])(output)
    proj = jnp.where(spec_section, spec_proj, prog_proj)
    unit, inverse, key = embed_rows(tops.reshape(sample_rows, width), proj)
    swap = shift_pairs("section", [(top_section, last_section), (last_section, top_section)])
    partner_key = swap(key)
    others = gather_rows(partner_key, "blk")
    scores = logit_scale * lax.dot_general(
        key, others, (((1,), (1,)), ((), ())), preferred_element_type=jnp.float32
    )
    row_max = jnp.max(scores, axis=1, keepdims=True)
    lse = row_max + jnp.log(jnp.sum(jnp.exp(scores - row_max), axis=1, keepdims=True))
    lse_down = shift_pairs("section", [(last_section, top_section)])(lse)
    lse_all = gather_rows(lse_down, "blk").reshape(1, -1)
    shift = jnp.where(spec_section, lse, lse_all)
    probs = jnp.exp(scores - shift).astype(jnp.bfloat16)
    dkey = logit_scale * (
        jnp.dot(probs, others, preferred_element_type=jnp.float32)
        - partner_key.astype(jnp.float32)
    )
    top_grad = embed_back(dkey, unit, inverse, proj).reshape(MICRO, micro_rows, width)
    saved_scaled = blank
    saved_dmixed = blank
    starts_grad = section_index >= top_section
    backward_offset = jnp.where(starts_grad, 0, top_section - section_index)
    incoming = jnp.zeros((micro_rows, width), jnp.bfloat16)
    for moment in range(MICRO + top_section):
        done = moment - 1
        senders = [s for s in range(1, top_section + 1) if 0 <= done - (top_section - s) < MICRO]
        if senders:
            incoming = shift_pairs("section", [(s, s - 1) for s in senders])(dhidden)
        micro_index = moment - backward_offset
        in_range = (micro_index >= 0) & (micro_index < MICRO)
        clipped = jnp.clip(micro_index, 0, MICRO - 1)
        upstream = jnp.where(
            starts_grad, lax.dynamic_index_in_dim(top_grad, clipped, 0, keepdims=False), incoming
        )
        hidden = lax.dynamic_index_in_dim(saved_inputs, clipped, 0, keepdims=False)
        dhidden, scaled, dmixed = layer_backward(hidden, upstream, layer_weights, gain)
        saved_scaled = keep_where(saved_scaled, scaled, clipped, in_range)
        saved_dmixed = keep_where(saved_dmixed, dmixed, clipped, in_range)
    scaled_all = saved_scaled.reshape(sample_rows, width)
    dmixed_all = saved_dmixed.reshape(sample_rows, width)
    partial = lax.dot_general(
        scaled_all, dmixed_all, (((0,), (0,)), ((), ())), preferred_element_type=jnp.float32
    )
    count = lax.axis_size("blk")
    pieces = partial.astype(jnp.bfloat16).reshape(count, width // count, width)
    landed = lax.all_to_all(pieces, "blk", 0, 0, tiled=True)
    return jnp.sum(landed.astype(jnp.float32), axis=0)


def solution(mesh):
    return jax.shard_map(
        local,
        mesh=mesh,
        in_specs=(
            P("blk", None),
            P("blk", None),
            P(),
            P(),
            P("section", None),
            P("section", None),
            P(),
            P(),
        ),
        out_specs=P(("section", "blk"), None),
        check_vma=False,
    )
```

```python
import jax
import jax.numpy as jnp
from jax import lax
from jax.sharding import PartitionSpec as P

L = 256
MICRO = 1
DIGIT = 32


logit_scale = 30.0
norm_eps = 1e-06


def shift_pairs(axis, pairs):
    return lambda value: lax.ppermute(value, axis, pairs)


def gather_rows(value, axis):
    count = lax.axis_size(axis)
    spread = jnp.broadcast_to(value[None], (count,) + value.shape)
    got = lax.all_to_all(spread, axis, 0, 0, tiled=True)
    return got.reshape((count * value.shape[0],) + value.shape[1:])


def layer_parts(hidden, weight, gain):
    wide = hidden.astype(jnp.float32)
    inverse = lax.rsqrt(jnp.mean(wide * wide, axis=1, keepdims=True) + norm_eps)
    normed = wide * inverse
    scaled = (normed * gain).astype(jnp.bfloat16)
    mixed = jnp.dot(scaled, weight, preferred_element_type=jnp.float32)
    return (wide, inverse, normed, scaled, mixed)


def layer_forward(hidden, weight, gain):
    wide, inverse, normed, scaled, mixed = layer_parts(hidden, weight, gain)
    return (wide + mixed * jax.nn.sigmoid(mixed)).astype(jnp.bfloat16)


def layer_backward(hidden, upstream, weight, gain):
    wide, inverse, normed, scaled, mixed = layer_parts(hidden, weight, gain)
    sigma = jax.nn.sigmoid(mixed)
    up_wide = upstream.astype(jnp.float32)
    dmixed = (up_wide * sigma * (1.0 + mixed * (1.0 - sigma))).astype(jnp.bfloat16)
    dnormed = (
        lax.dot_general(
            dmixed, weight, (((1,), (1,)), ((), ())), preferred_element_type=jnp.float32
        )
        * gain
    )
    dhidden = (
        up_wide + inverse * (dnormed - normed * jnp.mean(dnormed * normed, axis=1, keepdims=True))
    ).astype(jnp.bfloat16)
    return (dhidden, scaled, dmixed)


def embed_rows(hidden, proj):
    emb = jnp.dot(hidden, proj, preferred_element_type=jnp.float32)
    inverse = lax.rsqrt(jnp.sum(emb * emb, axis=1, keepdims=True) + norm_eps)
    unit = emb * inverse
    return (unit, inverse, unit.astype(jnp.bfloat16))


def embed_back(dkey, unit, inverse, proj):
    demb = (inverse * (dkey - unit * jnp.sum(unit * dkey, axis=1, keepdims=True))).astype(
        jnp.bfloat16
    )
    return lax.dot_general(
        demb, proj, (((1,), (1,)), ((), ())), preferred_element_type=jnp.float32
    ).astype(jnp.bfloat16)


def keep_where(buffer, value, index, valid):
    previous = lax.dynamic_index_in_dim(buffer, index, 0, keepdims=False)
    return lax.dynamic_update_index_in_dim(buffer, jnp.where(valid, value, previous), index, 0)


def local(prog_ids, spec_ids, prog_table, spec_table, layer_weights, gains, prog_proj, spec_proj):
    section_index = lax.axis_index("section")
    last_section = lax.axis_size("section") - 1
    top_section = last_section - 1
    spec_section = section_index == last_section
    token_ids = jnp.where(spec_section, spec_ids, prog_ids)
    table = jnp.where(spec_section, spec_table, prog_table)
    vocab = table.shape[0]
    high = (token_ids // DIGIT)[:, :, None] == jnp.arange(vocab // DIGIT, dtype=jnp.int32)
    low = (token_ids % DIGIT)[:, :, None] == jnp.arange(DIGIT, dtype=jnp.int32)
    counts = jnp.einsum(
        "bth,btl->bhl",
        high.astype(jnp.bfloat16),
        low.astype(jnp.bfloat16),
        preferred_element_type=jnp.float32,
    ).reshape(token_ids.shape[0], vocab).astype(jnp.bfloat16)
    sample_rows = prog_ids.shape[0]
    micro_rows = sample_rows // MICRO
    width = layer_weights.shape[1]
    first_inputs = (jnp.dot(counts, table, preferred_element_type=jnp.float32) * (1.0 / L)).astype(
        jnp.bfloat16
    )
    first_inputs = first_inputs.reshape(MICRO, micro_rows, width)
    gain = gains[0]
    blank = jnp.zeros((MICRO, micro_rows, width), jnp.bfloat16)
    saved_inputs = blank
    tops = blank
    received = jnp.zeros((micro_rows, width), jnp.bfloat16)
    forward_offset = jnp.where(spec_section, 0, section_index)
    takes_bag = spec_section | (section_index == 0)
    for moment in range(MICRO + top_section):
        micro_index = moment - forward_offset
        in_range = (micro_index >= 0) & (micro_index < MICRO)
        clipped = jnp.clip(micro_index, 0, MICRO - 1)
        from_bag = lax.dynamic_index_in_dim(first_inputs, clipped, 0, keepdims=False)
        current = jnp.where(takes_bag, from_bag, received)
        saved_inputs = keep_where(saved_inputs, current, clipped, in_range)
        output = layer_forward(current, layer_weights, gain)
        tops = keep_where(tops, output, clipped, in_range)
        senders = [s for s in range(top_section) if 0 <= moment - s < MICRO]
        if senders:
            received = shift_pairs("section", [(s, s + 1) for s in senders])(output)
    proj = jnp.where(spec_section, spec_proj, prog_proj)
    unit, inverse, key = embed_rows(tops.reshape(sample_rows, width), proj)
    swap = shift_pairs("section", [(top_section, last_section), (last_section, top_section)])
    partner_key = swap(key)
    others = gather_rows(partner_key, "blk")
    scores = logit_scale * lax.dot_general(
        key, others, (((1,), (1,)), ((), ())), preferred_element_type=jnp.float32
    )
    row_max = jnp.max(scores, axis=1, keepdims=True)
    lse = row_max + jnp.log(jnp.sum(jnp.exp(scores - row_max), axis=1, keepdims=True))
    lse_down = shift_pairs("section", [(last_section, top_section)])(lse)
    lse_all = gather_rows(lse_down, "blk").reshape(1, -1)
    shift = jnp.where(spec_section, lse, lse_all)
    probs = jnp.exp(scores - shift).astype(jnp.bfloat16)
    dkey = logit_scale * (
        jnp.dot(probs, others, preferred_element_type=jnp.float32)
        - partner_key.astype(jnp.float32)
    )
    top_grad = embed_back(dkey, unit, inverse, proj).reshape(MICRO, micro_rows, width)
    saved_scaled = blank
    saved_dmixed = blank
    starts_grad = section_index >= top_section
    backward_offset = jnp.where(starts_grad, 0, top_section - section_index)
    incoming = jnp.zeros((micro_rows, width), jnp.bfloat16)
    for moment in range(MICRO + top_section):
        done = moment - 1
        senders = [s for s in range(1, top_section + 1) if 0 <= done - (top_section - s) < MICRO]
        if senders:
            incoming = shift_pairs("section", [(s, s - 1) for s in senders])(dhidden)
        micro_index = moment - backward_offset
        in_range = (micro_index >= 0) & (micro_index < MICRO)
        clipped = jnp.clip(micro_index, 0, MICRO - 1)
        upstream = jnp.where(
            starts_grad, lax.dynamic_index_in_dim(top_grad, clipped, 0, keepdims=False), incoming
        )
        hidden = lax.dynamic_index_in_dim(saved_inputs, clipped, 0, keepdims=False)
        dhidden, scaled, dmixed = layer_backward(hidden, upstream, layer_weights, gain)
        saved_scaled = keep_where(saved_scaled, scaled, clipped, in_range)
        saved_dmixed = keep_where(saved_dmixed, dmixed, clipped, in_range)
    scaled_all = saved_scaled.reshape(sample_rows, width)
    dmixed_all = saved_dmixed.reshape(sample_rows, width)
    partial = lax.dot_general(
        scaled_all, dmixed_all, (((0,), (0,)), ((), ())), preferred_element_type=jnp.float32
    )
    count = lax.axis_size("blk")
    pieces = partial.astype(jnp.bfloat16).reshape(count, width // count, width)
    landed = lax.all_to_all(pieces, "blk", 0, 0, tiled=True)
    return jnp.sum(landed.astype(jnp.float32), axis=0)


def solution(mesh):
    return jax.shard_map(
        local,
        mesh=mesh,
        in_specs=(
            P("blk", None),
            P("blk", None),
            P(),
            P(),
            P("section", None),
            P("section", None),
            P(),
            P(),
        ),
        out_specs=P(("section", "blk"), None),
        check_vma=False,
    )
```

```python
import jax
import jax.numpy as jnp
from jax import lax
from jax.sharding import PartitionSpec as P

L = 256
MICRO = 1
DIGIT = 32


logit_scale = 30.0
norm_eps = 1e-06


def shift_pairs(axis, pairs):
    return lambda value: lax.ppermute(value, axis, pairs)


def gather_rows(value, axis):
    count = lax.axis_size(axis)
    spread = jnp.broadcast_to(value[None], (count,) + value.shape)
    got = lax.all_to_all(spread, axis, 0, 0, tiled=True)
    return got.reshape((count * value.shape[0],) + value.shape[1:])


def layer_parts(hidden, weight, gain):
    wide = hidden.astype(jnp.float32)
    inverse = lax.rsqrt(jnp.mean(wide * wide, axis=1, keepdims=True) + norm_eps)
    normed = wide * inverse
    scaled = (normed * gain).astype(jnp.bfloat16)
    mixed = jnp.dot(scaled, weight, preferred_element_type=jnp.float32)
    return (wide, inverse, normed, scaled, mixed)


def layer_forward(hidden, weight, gain):
    wide, inverse, normed, scaled, mixed = layer_parts(hidden, weight, gain)
    return ((wide + mixed * jax.nn.sigmoid(mixed)).astype(jnp.bfloat16), mixed)


def layer_backward(hidden, upstream, weight, gain, mixed):
    wide = hidden.astype(jnp.float32)
    inverse = lax.rsqrt(jnp.mean(wide * wide, axis=1, keepdims=True) + norm_eps)
    normed = wide * inverse
    scaled = (normed * gain).astype(jnp.bfloat16)
    sigma = jax.nn.sigmoid(mixed)
    up_wide = upstream.astype(jnp.float32)
    dmixed = (up_wide * sigma * (1.0 + mixed * (1.0 - sigma))).astype(jnp.bfloat16)
    dnormed = (
        lax.dot_general(
            dmixed, weight, (((1,), (1,)), ((), ())), preferred_element_type=jnp.float32
        )
        * gain
    )
    dhidden = (
        up_wide + inverse * (dnormed - normed * jnp.mean(dnormed * normed, axis=1, keepdims=True))
    ).astype(jnp.bfloat16)
    return (dhidden, scaled, dmixed)


def embed_rows(hidden, proj):
    emb = jnp.dot(hidden, proj, preferred_element_type=jnp.float32)
    inverse = lax.rsqrt(jnp.sum(emb * emb, axis=1, keepdims=True) + norm_eps)
    unit = emb * inverse
    return (unit, inverse, unit.astype(jnp.bfloat16))


def embed_back(dkey, unit, inverse, proj):
    demb = (inverse * (dkey - unit * jnp.sum(unit * dkey, axis=1, keepdims=True))).astype(
        jnp.bfloat16
    )
    return lax.dot_general(
        demb, proj, (((1,), (1,)), ((), ())), preferred_element_type=jnp.float32
    ).astype(jnp.bfloat16)


def keep_where(buffer, value, index, valid):
    previous = lax.dynamic_index_in_dim(buffer, index, 0, keepdims=False)
    return lax.dynamic_update_index_in_dim(buffer, jnp.where(valid, value, previous), index, 0)


def local(prog_ids, spec_ids, prog_table, spec_table, layer_weights, gains, prog_proj, spec_proj):
    section_index = lax.axis_index("section")
    last_section = lax.axis_size("section") - 1
    top_section = last_section - 1
    spec_section = section_index == last_section
    token_ids = jnp.where(spec_section, spec_ids, prog_ids)
    table = jnp.where(spec_section, spec_table, prog_table)
    vocab = table.shape[0]
    high = (token_ids // DIGIT)[:, :, None] == jnp.arange(vocab // DIGIT, dtype=jnp.int32)
    low = (token_ids % DIGIT)[:, :, None] == jnp.arange(DIGIT, dtype=jnp.int32)
    counts = jnp.einsum(
        "bth,btl->bhl",
        high.astype(jnp.bfloat16),
        low.astype(jnp.bfloat16),
        preferred_element_type=jnp.float32,
    ).reshape(token_ids.shape[0], vocab).astype(jnp.bfloat16)
    sample_rows = prog_ids.shape[0]
    micro_rows = sample_rows // MICRO
    width = layer_weights.shape[1]
    first_inputs = (jnp.dot(counts, table, preferred_element_type=jnp.float32) * (1.0 / L)).astype(
        jnp.bfloat16
    )
    first_inputs = first_inputs.reshape(MICRO, micro_rows, width)
    gain = gains[0]
    blank = jnp.zeros((MICRO, micro_rows, width), jnp.bfloat16)
    saved_inputs = blank
    tops = blank
    saved_mixed = jnp.zeros((MICRO, micro_rows, width), jnp.float32)
    received = jnp.zeros((micro_rows, width), jnp.bfloat16)
    forward_offset = jnp.where(spec_section, 0, section_index)
    takes_bag = spec_section | (section_index == 0)
    for moment in range(MICRO + top_section):
        micro_index = moment - forward_offset
        in_range = (micro_index >= 0) & (micro_index < MICRO)
        clipped = jnp.clip(micro_index, 0, MICRO - 1)
        from_bag = lax.dynamic_index_in_dim(first_inputs, clipped, 0, keepdims=False)
        current = jnp.where(takes_bag, from_bag, received)
        saved_inputs = keep_where(saved_inputs, current, clipped, in_range)
        output, mixed = layer_forward(current, layer_weights, gain)
        tops = keep_where(tops, output, clipped, in_range)
        saved_mixed = keep_where(saved_mixed, mixed, clipped, in_range)
        senders = [s for s in range(top_section) if 0 <= moment - s < MICRO]
        if senders:
            received = shift_pairs("section", [(s, s + 1) for s in senders])(output)
    proj = jnp.where(spec_section, spec_proj, prog_proj)
    unit, inverse, key = embed_rows(tops.reshape(sample_rows, width), proj)
    swap = shift_pairs("section", [(top_section, last_section), (last_section, top_section)])
    partner_key = swap(key)
    others = gather_rows(partner_key, "blk")
    scores = logit_scale * lax.dot_general(
        key, others, (((1,), (1,)), ((), ())), preferred_element_type=jnp.float32
    )
    row_max = jnp.max(scores, axis=1, keepdims=True)
    lse = row_max + jnp.log(jnp.sum(jnp.exp(scores - row_max), axis=1, keepdims=True))
    lse_down = shift_pairs("section", [(last_section, top_section)])(lse)
    lse_all = gather_rows(lse_down, "blk").reshape(1, -1)
    shift = jnp.where(spec_section, lse, lse_all)
    probs = jnp.exp(scores - shift).astype(jnp.bfloat16)
    dkey = logit_scale * (
        jnp.dot(probs, others, preferred_element_type=jnp.float32)
        - partner_key.astype(jnp.float32)
    )
    top_grad = embed_back(dkey, unit, inverse, proj).reshape(MICRO, micro_rows, width)
    saved_scaled = blank
    saved_dmixed = blank
    starts_grad = section_index >= top_section
    backward_offset = jnp.where(starts_grad, 0, top_section - section_index)
    incoming = jnp.zeros((micro_rows, width), jnp.bfloat16)
    for moment in range(MICRO + top_section):
        done = moment - 1
        senders = [s for s in range(1, top_section + 1) if 0 <= done - (top_section - s) < MICRO]
        if senders:
            incoming = shift_pairs("section", [(s, s - 1) for s in senders])(dhidden)
        micro_index = moment - backward_offset
        in_range = (micro_index >= 0) & (micro_index < MICRO)
        clipped = jnp.clip(micro_index, 0, MICRO - 1)
        upstream = jnp.where(
            starts_grad, lax.dynamic_index_in_dim(top_grad, clipped, 0, keepdims=False), incoming
        )
        hidden = lax.dynamic_index_in_dim(saved_inputs, clipped, 0, keepdims=False)
        mixed = lax.dynamic_index_in_dim(saved_mixed, clipped, 0, keepdims=False)
        dhidden, scaled, dmixed = layer_backward(hidden, upstream, layer_weights, gain, mixed)
        saved_scaled = keep_where(saved_scaled, scaled, clipped, in_range)
        saved_dmixed = keep_where(saved_dmixed, dmixed, clipped, in_range)
    scaled_all = saved_scaled.reshape(sample_rows, width)
    dmixed_all = saved_dmixed.reshape(sample_rows, width)
    partial = lax.dot_general(
        scaled_all, dmixed_all, (((0,), (0,)), ((), ())), preferred_element_type=jnp.float32
    )
    count = lax.axis_size("blk")
    pieces = partial.astype(jnp.bfloat16).reshape(count, width // count, width)
    landed = lax.all_to_all(pieces, "blk", 0, 0, tiled=True)
    return jnp.sum(landed.astype(jnp.float32), axis=0)


def solution(mesh):
    return jax.shard_map(
        local,
        mesh=mesh,
        in_specs=(
            P("blk", None),
            P("blk", None),
            P(),
            P(),
            P("section", None),
            P("section", None),
            P(),
            P(),
        ),
        out_specs=P(("section", "blk"), None),
        check_vma=False,
    )
```

```python
import jax
import jax.numpy as jnp
from jax import lax
from jax.sharding import PartitionSpec as P

L = 256
MICRO = 2
DIGIT = 32


logit_scale = 30.0
norm_eps = 1e-06


def shift_pairs(axis, pairs):
    return lambda value: lax.ppermute(value, axis, pairs)


def gather_rows(value, axis):
    count = lax.axis_size(axis)
    spread = jnp.broadcast_to(value[None], (count,) + value.shape)
    got = lax.all_to_all(spread, axis, 0, 0, tiled=True)
    return got.reshape((count * value.shape[0],) + value.shape[1:])


def layer_parts(hidden, weight, gain):
    wide = hidden.astype(jnp.float32)
    inverse = lax.rsqrt(jnp.mean(wide * wide, axis=1, keepdims=True) + norm_eps)
    normed = wide * inverse
    scaled = (normed * gain).astype(jnp.bfloat16)
    mixed = jnp.dot(scaled, weight, preferred_element_type=jnp.float32)
    return (wide, inverse, normed, scaled, mixed)


def layer_forward(hidden, weight, gain):
    wide, inverse, normed, scaled, mixed = layer_parts(hidden, weight, gain)
    return ((wide + mixed * jax.nn.sigmoid(mixed)).astype(jnp.bfloat16), mixed)


def layer_backward(hidden, upstream, weight, gain, mixed):
    wide = hidden.astype(jnp.float32)
    inverse = lax.rsqrt(jnp.mean(wide * wide, axis=1, keepdims=True) + norm_eps)
    normed = wide * inverse
    scaled = (normed * gain).astype(jnp.bfloat16)
    sigma = jax.nn.sigmoid(mixed)
    up_wide = upstream.astype(jnp.float32)
    dmixed = (up_wide * sigma * (1.0 + mixed * (1.0 - sigma))).astype(jnp.bfloat16)
    dnormed = (
        lax.dot_general(
            dmixed, weight, (((1,), (1,)), ((), ())), preferred_element_type=jnp.float32
        )
        * gain
    )
    dhidden = (
        up_wide + inverse * (dnormed - normed * jnp.mean(dnormed * normed, axis=1, keepdims=True))
    ).astype(jnp.bfloat16)
    return (dhidden, scaled, dmixed)


def embed_rows(hidden, proj):
    emb = jnp.dot(hidden, proj, preferred_element_type=jnp.float32)
    inverse = lax.rsqrt(jnp.sum(emb * emb, axis=1, keepdims=True) + norm_eps)
    unit = emb * inverse
    return (unit, inverse, unit.astype(jnp.bfloat16))


def embed_back(dkey, unit, inverse, proj):
    demb = (inverse * (dkey - unit * jnp.sum(unit * dkey, axis=1, keepdims=True))).astype(
        jnp.bfloat16
    )
    return lax.dot_general(
        demb, proj, (((1,), (1,)), ((), ())), preferred_element_type=jnp.float32
    ).astype(jnp.bfloat16)


def keep_where(buffer, value, index, valid):
    previous = lax.dynamic_index_in_dim(buffer, index, 0, keepdims=False)
    return lax.dynamic_update_index_in_dim(buffer, jnp.where(valid, value, previous), index, 0)


def local(prog_ids, spec_ids, prog_table, spec_table, layer_weights, gains, prog_proj, spec_proj):
    section_index = lax.axis_index("section")
    last_section = lax.axis_size("section") - 1
    top_section = last_section - 1
    spec_section = section_index == last_section
    token_ids = jnp.where(spec_section, spec_ids, prog_ids)
    table = jnp.where(spec_section, spec_table, prog_table)
    vocab = table.shape[0]
    high = (token_ids // DIGIT)[:, :, None] == jnp.arange(vocab // DIGIT, dtype=jnp.int32)
    low = (token_ids % DIGIT)[:, :, None] == jnp.arange(DIGIT, dtype=jnp.int32)
    counts = jnp.einsum(
        "bth,btl->bhl",
        high.astype(jnp.bfloat16),
        low.astype(jnp.bfloat16),
        preferred_element_type=jnp.float32,
    ).reshape(token_ids.shape[0], vocab).astype(jnp.bfloat16)
    sample_rows = prog_ids.shape[0]
    micro_rows = sample_rows // MICRO
    width = layer_weights.shape[1]
    first_inputs = (jnp.dot(counts, table, preferred_element_type=jnp.float32) * (1.0 / L)).astype(
        jnp.bfloat16
    )
    first_inputs = first_inputs.reshape(MICRO, micro_rows, width)
    gain = gains[0]
    blank = jnp.zeros((MICRO, micro_rows, width), jnp.bfloat16)
    saved_inputs = blank
    tops = blank
    saved_mixed = jnp.zeros((MICRO, micro_rows, width), jnp.float32)
    received = jnp.zeros((micro_rows, width), jnp.bfloat16)
    forward_offset = jnp.where(spec_section, 0, section_index)
    takes_bag = spec_section | (section_index == 0)
    for moment in range(MICRO + top_section):
        micro_index = moment - forward_offset
        in_range = (micro_index >= 0) & (micro_index < MICRO)
        clipped = jnp.clip(micro_index, 0, MICRO - 1)
        from_bag = lax.dynamic_index_in_dim(first_inputs, clipped, 0, keepdims=False)
        current = jnp.where(takes_bag, from_bag, received)
        saved_inputs = keep_where(saved_inputs, current, clipped, in_range)
        output, mixed = layer_forward(current, layer_weights, gain)
        tops = keep_where(tops, output, clipped, in_range)
        saved_mixed = keep_where(saved_mixed, mixed, clipped, in_range)
        senders = [s for s in range(top_section) if 0 <= moment - s < MICRO]
        if senders:
            received = shift_pairs("section", [(s, s + 1) for s in senders])(output)
    proj = jnp.where(spec_section, spec_proj, prog_proj)
    unit, inverse, key = embed_rows(tops.reshape(sample_rows, width), proj)
    swap = shift_pairs("section", [(top_section, last_section), (last_section, top_section)])
    partner_key = swap(key)
    others = gather_rows(partner_key, "blk")
    scores = logit_scale * lax.dot_general(
        key, others, (((1,), (1,)), ((), ())), preferred_element_type=jnp.float32
    )
    row_max = jnp.max(scores, axis=1, keepdims=True)
    lse = row_max + jnp.log(jnp.sum(jnp.exp(scores - row_max), axis=1, keepdims=True))
    lse_down = shift_pairs("section", [(last_section, top_section)])(lse)
    lse_all = gather_rows(lse_down, "blk").reshape(1, -1)
    shift = jnp.where(spec_section, lse, lse_all)
    probs = jnp.exp(scores - shift).astype(jnp.bfloat16)
    dkey = logit_scale * (
        jnp.dot(probs, others, preferred_element_type=jnp.float32)
        - partner_key.astype(jnp.float32)
    )
    top_grad = embed_back(dkey, unit, inverse, proj).reshape(MICRO, micro_rows, width)
    saved_scaled = blank
    saved_dmixed = blank
    starts_grad = section_index >= top_section
    backward_offset = jnp.where(starts_grad, 0, top_section - section_index)
    incoming = jnp.zeros((micro_rows, width), jnp.bfloat16)
    for moment in range(MICRO + top_section):
        done = moment - 1
        senders = [s for s in range(1, top_section + 1) if 0 <= done - (top_section - s) < MICRO]
        if senders:
            incoming = shift_pairs("section", [(s, s - 1) for s in senders])(dhidden)
        micro_index = moment - backward_offset
        in_range = (micro_index >= 0) & (micro_index < MICRO)
        clipped = jnp.clip(micro_index, 0, MICRO - 1)
        upstream = jnp.where(
            starts_grad, lax.dynamic_index_in_dim(top_grad, clipped, 0, keepdims=False), incoming
        )
        hidden = lax.dynamic_index_in_dim(saved_inputs, clipped, 0, keepdims=False)
        mixed = lax.dynamic_index_in_dim(saved_mixed, clipped, 0, keepdims=False)
        dhidden, scaled, dmixed = layer_backward(hidden, upstream, layer_weights, gain, mixed)
        saved_scaled = keep_where(saved_scaled, scaled, clipped, in_range)
        saved_dmixed = keep_where(saved_dmixed, dmixed, clipped, in_range)
    scaled_all = saved_scaled.reshape(sample_rows, width)
    dmixed_all = saved_dmixed.reshape(sample_rows, width)
    partial = lax.dot_general(
        scaled_all, dmixed_all, (((0,), (0,)), ((), ())), preferred_element_type=jnp.float32
    )
    count = lax.axis_size("blk")
    pieces = partial.astype(jnp.bfloat16).reshape(count, width // count, width)
    landed = lax.all_to_all(pieces, "blk", 0, 0, tiled=True)
    return jnp.sum(landed.astype(jnp.float32), axis=0)


def solution(mesh):
    return jax.shard_map(
        local,
        mesh=mesh,
        in_specs=(
            P("blk", None),
            P("blk", None),
            P(),
            P(),
            P("section", None),
            P("section", None),
            P(),
            P(),
        ),
        out_specs=P(("section", "blk"), None),
        check_vma=False,
    )
```

```python
import jax
import jax.numpy as jnp
from jax import lax
from jax.sharding import PartitionSpec as P

L = 256
MICRO = 1
DIGIT = 32


logit_scale = 30.0
norm_eps = 1e-06


def shift_pairs(axis, pairs):
    return lambda value: lax.ppermute(value, axis, pairs)


def gather_rows(value, axis):
    count = lax.axis_size(axis)
    spread = jnp.broadcast_to(value[None], (count,) + value.shape)
    got = lax.all_to_all(spread, axis, 0, 0, tiled=True)
    return got.reshape((count * value.shape[0],) + value.shape[1:])


def layer_parts(hidden, weight, gain):
    wide = hidden.astype(jnp.float32)
    inverse = lax.rsqrt(jnp.mean(wide * wide, axis=1, keepdims=True) + norm_eps)
    normed = wide * inverse
    scaled = (normed * gain).astype(jnp.bfloat16)
    mixed = jnp.dot(scaled, weight, preferred_element_type=jnp.float32)
    return (wide, inverse, normed, scaled, mixed)


def layer_forward(hidden, weight, gain):
    wide, inverse, normed, scaled, mixed = layer_parts(hidden, weight, gain)
    return ((wide + mixed * jax.nn.sigmoid(mixed)).astype(jnp.bfloat16), mixed, scaled, inverse)


def layer_backward(hidden, upstream, weight, gain, mixed, scaled, inverse):
    normed = hidden.astype(jnp.float32) * inverse
    sigma = jax.nn.sigmoid(mixed)
    up_wide = upstream.astype(jnp.float32)
    dmixed = (up_wide * sigma * (1.0 + mixed * (1.0 - sigma))).astype(jnp.bfloat16)
    dnormed = (
        lax.dot_general(
            dmixed, weight, (((1,), (1,)), ((), ())), preferred_element_type=jnp.float32
        )
        * gain
    )
    dhidden = (
        up_wide + inverse * (dnormed - normed * jnp.mean(dnormed * normed, axis=1, keepdims=True))
    ).astype(jnp.bfloat16)
    return (dhidden, scaled, dmixed)


def embed_rows(hidden, proj):
    emb = jnp.dot(hidden, proj, preferred_element_type=jnp.float32)
    inverse = lax.rsqrt(jnp.sum(emb * emb, axis=1, keepdims=True) + norm_eps)
    unit = emb * inverse
    return (unit, inverse, unit.astype(jnp.bfloat16))


def embed_back(dkey, unit, inverse, proj):
    demb = (inverse * (dkey - unit * jnp.sum(unit * dkey, axis=1, keepdims=True))).astype(
        jnp.bfloat16
    )
    return lax.dot_general(
        demb, proj, (((1,), (1,)), ((), ())), preferred_element_type=jnp.float32
    ).astype(jnp.bfloat16)


def keep_where(buffer, value, index, valid):
    previous = lax.dynamic_index_in_dim(buffer, index, 0, keepdims=False)
    return lax.dynamic_update_index_in_dim(buffer, jnp.where(valid, value, previous), index, 0)


def local(prog_ids, spec_ids, prog_table, spec_table, layer_weights, gains, prog_proj, spec_proj):
    section_index = lax.axis_index("section")
    last_section = lax.axis_size("section") - 1
    top_section = last_section - 1
    spec_section = section_index == last_section
    token_ids = jnp.where(spec_section, spec_ids, prog_ids)
    table = jnp.where(spec_section, spec_table, prog_table)
    vocab = table.shape[0]
    high = (token_ids // DIGIT)[:, :, None] == jnp.arange(vocab // DIGIT, dtype=jnp.int32)
    low = (token_ids % DIGIT)[:, :, None] == jnp.arange(DIGIT, dtype=jnp.int32)
    counts = jnp.einsum(
        "bth,btl->bhl",
        high.astype(jnp.bfloat16),
        low.astype(jnp.bfloat16),
        preferred_element_type=jnp.float32,
    ).reshape(token_ids.shape[0], vocab).astype(jnp.bfloat16)
    sample_rows = prog_ids.shape[0]
    micro_rows = sample_rows // MICRO
    width = layer_weights.shape[1]
    first_inputs = (jnp.dot(counts, table, preferred_element_type=jnp.float32) * (1.0 / L)).astype(
        jnp.bfloat16
    )
    first_inputs = first_inputs.reshape(MICRO, micro_rows, width)
    gain = gains[0]
    blank = jnp.zeros((MICRO, micro_rows, width), jnp.bfloat16)
    saved_inputs = blank
    tops = blank
    saved_mixed = jnp.zeros((MICRO, micro_rows, width), jnp.float32)
    kept_scaled = blank
    saved_inverse = jnp.zeros((MICRO, micro_rows, 1), jnp.float32)
    received = jnp.zeros((micro_rows, width), jnp.bfloat16)
    forward_offset = jnp.where(spec_section, 0, section_index)
    takes_bag = spec_section | (section_index == 0)
    for moment in range(MICRO + top_section):
        micro_index = moment - forward_offset
        in_range = (micro_index >= 0) & (micro_index < MICRO)
        clipped = jnp.clip(micro_index, 0, MICRO - 1)
        from_bag = lax.dynamic_index_in_dim(first_inputs, clipped, 0, keepdims=False)
        current = jnp.where(takes_bag, from_bag, received)
        saved_inputs = keep_where(saved_inputs, current, clipped, in_range)
        output, mixed, scaled, inverse = layer_forward(current, layer_weights, gain)
        tops = keep_where(tops, output, clipped, in_range)
        saved_mixed = keep_where(saved_mixed, mixed, clipped, in_range)
        kept_scaled = keep_where(kept_scaled, scaled, clipped, in_range)
        saved_inverse = keep_where(saved_inverse, inverse, clipped, in_range)
        senders = [s for s in range(top_section) if 0 <= moment - s < MICRO]
        if senders:
            received = shift_pairs("section", [(s, s + 1) for s in senders])(output)
    proj = jnp.where(spec_section, spec_proj, prog_proj)
    unit, inverse, key = embed_rows(tops.reshape(sample_rows, width), proj)
    swap = shift_pairs("section", [(top_section, last_section), (last_section, top_section)])
    partner_key = swap(key)
    others = gather_rows(partner_key, "blk")
    scores = logit_scale * lax.dot_general(
        key, others, (((1,), (1,)), ((), ())), preferred_element_type=jnp.float32
    )
    row_max = jnp.max(scores, axis=1, keepdims=True)
    lse = row_max + jnp.log(jnp.sum(jnp.exp(scores - row_max), axis=1, keepdims=True))
    lse_down = shift_pairs("section", [(last_section, top_section)])(lse)
    lse_all = gather_rows(lse_down, "blk").reshape(1, -1)
    shift = jnp.where(spec_section, lse, lse_all)
    probs = jnp.exp(scores - shift).astype(jnp.bfloat16)
    dkey = logit_scale * (
        jnp.dot(probs, others, preferred_element_type=jnp.float32)
        - partner_key.astype(jnp.float32)
    )
    top_grad = embed_back(dkey, unit, inverse, proj).reshape(MICRO, micro_rows, width)
    saved_scaled = blank
    saved_dmixed = blank
    starts_grad = section_index >= top_section
    backward_offset = jnp.where(starts_grad, 0, top_section - section_index)
    incoming = jnp.zeros((micro_rows, width), jnp.bfloat16)
    for moment in range(MICRO + top_section):
        done = moment - 1
        senders = [s for s in range(1, top_section + 1) if 0 <= done - (top_section - s) < MICRO]
        if senders:
            incoming = shift_pairs("section", [(s, s - 1) for s in senders])(dhidden)
        micro_index = moment - backward_offset
        in_range = (micro_index >= 0) & (micro_index < MICRO)
        clipped = jnp.clip(micro_index, 0, MICRO - 1)
        upstream = jnp.where(
            starts_grad, lax.dynamic_index_in_dim(top_grad, clipped, 0, keepdims=False), incoming
        )
        hidden = lax.dynamic_index_in_dim(saved_inputs, clipped, 0, keepdims=False)
        mixed = lax.dynamic_index_in_dim(saved_mixed, clipped, 0, keepdims=False)
        scaled = lax.dynamic_index_in_dim(kept_scaled, clipped, 0, keepdims=False)
        inverse = lax.dynamic_index_in_dim(saved_inverse, clipped, 0, keepdims=False)
        dhidden, scaled, dmixed = layer_backward(
            hidden, upstream, layer_weights, gain, mixed, scaled, inverse
        )
        saved_scaled = keep_where(saved_scaled, scaled, clipped, in_range)
        saved_dmixed = keep_where(saved_dmixed, dmixed, clipped, in_range)
    scaled_all = saved_scaled.reshape(sample_rows, width)
    dmixed_all = saved_dmixed.reshape(sample_rows, width)
    partial = lax.dot_general(
        scaled_all, dmixed_all, (((0,), (0,)), ((), ())), preferred_element_type=jnp.float32
    )
    count = lax.axis_size("blk")
    pieces = partial.astype(jnp.bfloat16).reshape(count, width // count, width)
    landed = lax.all_to_all(pieces, "blk", 0, 0, tiled=True)
    return jnp.sum(landed.astype(jnp.float32), axis=0)


def solution(mesh):
    return jax.shard_map(
        local,
        mesh=mesh,
        in_specs=(
            P("blk", None),
            P("blk", None),
            P(),
            P(),
            P("section", None),
            P("section", None),
            P(),
            P(),
        ),
        out_specs=P(("section", "blk"), None),
        check_vma=False,
    )
```

```python
import jax
import jax.numpy as jnp
from jax import lax
from jax.sharding import PartitionSpec as P

L = 256
MICRO = 1
DIGIT = 32


logit_scale = 30.0
norm_eps = 1e-06


def shift_pairs(axis, pairs):
    return lambda value: lax.ppermute(value, axis, pairs)


def hop(value, source, target, relay):
    if relay is None:
        return lax.ppermute(value, "section", [(source, target)])
    half = value.shape[0] // 2
    direct = lax.ppermute(value[:half], "section", [(source, target)])
    first = lax.ppermute(value[half:], "section", [(source, relay)])
    second = lax.ppermute(first, "section", [(relay, target)])
    return jnp.concatenate([direct, second], axis=0)


def gather_rows(value, axis):
    count = lax.axis_size(axis)
    spread = jnp.broadcast_to(value[None], (count,) + value.shape)
    got = lax.all_to_all(spread, axis, 0, 0, tiled=True)
    return got.reshape((count * value.shape[0],) + value.shape[1:])


def layer_parts(hidden, weight, gain):
    wide = hidden.astype(jnp.float32)
    inverse = lax.rsqrt(jnp.mean(wide * wide, axis=1, keepdims=True) + norm_eps)
    normed = wide * inverse
    scaled = (normed * gain).astype(jnp.bfloat16)
    mixed = jnp.dot(scaled, weight, preferred_element_type=jnp.float32)
    return (wide, inverse, normed, scaled, mixed)


def layer_forward(hidden, weight, gain):
    wide, inverse, normed, scaled, mixed = layer_parts(hidden, weight, gain)
    return ((wide + mixed * jax.nn.sigmoid(mixed)).astype(jnp.bfloat16), mixed)


def layer_backward(hidden, upstream, weight, gain, mixed):
    wide = hidden.astype(jnp.float32)
    inverse = lax.rsqrt(jnp.mean(wide * wide, axis=1, keepdims=True) + norm_eps)
    normed = wide * inverse
    scaled = (normed * gain).astype(jnp.bfloat16)
    sigma = jax.nn.sigmoid(mixed)
    up_wide = upstream.astype(jnp.float32)
    dmixed = (up_wide * sigma * (1.0 + mixed * (1.0 - sigma))).astype(jnp.bfloat16)
    dnormed = (
        lax.dot_general(
            dmixed, weight, (((1,), (1,)), ((), ())), preferred_element_type=jnp.float32
        )
        * gain
    )
    dhidden = (
        up_wide + inverse * (dnormed - normed * jnp.mean(dnormed * normed, axis=1, keepdims=True))
    ).astype(jnp.bfloat16)
    return (dhidden, scaled, dmixed)


def embed_rows(hidden, proj):
    emb = jnp.dot(hidden, proj, preferred_element_type=jnp.float32)
    inverse = lax.rsqrt(jnp.sum(emb * emb, axis=1, keepdims=True) + norm_eps)
    unit = emb * inverse
    return (unit, inverse, unit.astype(jnp.bfloat16))


def embed_back(dkey, unit, inverse, proj):
    demb = (inverse * (dkey - unit * jnp.sum(unit * dkey, axis=1, keepdims=True))).astype(
        jnp.bfloat16
    )
    return lax.dot_general(
        demb, proj, (((1,), (1,)), ((), ())), preferred_element_type=jnp.float32
    ).astype(jnp.bfloat16)


def keep_where(buffer, value, index, valid):
    previous = lax.dynamic_index_in_dim(buffer, index, 0, keepdims=False)
    return lax.dynamic_update_index_in_dim(buffer, jnp.where(valid, value, previous), index, 0)


def local(prog_ids, spec_ids, prog_table, spec_table, layer_weights, gains, prog_proj, spec_proj):
    section_index = lax.axis_index("section")
    last_section = lax.axis_size("section") - 1
    top_section = last_section - 1
    spec_section = section_index == last_section
    token_ids = jnp.where(spec_section, spec_ids, prog_ids)
    table = jnp.where(spec_section, spec_table, prog_table)
    vocab = table.shape[0]
    high = (token_ids // DIGIT)[:, :, None] == jnp.arange(vocab // DIGIT, dtype=jnp.int32)
    low = (token_ids % DIGIT)[:, :, None] == jnp.arange(DIGIT, dtype=jnp.int32)
    counts = jnp.einsum(
        "bth,btl->bhl",
        high.astype(jnp.bfloat16),
        low.astype(jnp.bfloat16),
        preferred_element_type=jnp.float32,
    ).reshape(token_ids.shape[0], vocab).astype(jnp.bfloat16)
    sample_rows = prog_ids.shape[0]
    micro_rows = sample_rows // MICRO
    width = layer_weights.shape[1]
    first_inputs = (jnp.dot(counts, table, preferred_element_type=jnp.float32) * (1.0 / L)).astype(
        jnp.bfloat16
    )
    first_inputs = first_inputs.reshape(MICRO, micro_rows, width)
    gain = gains[0]
    blank = jnp.zeros((MICRO, micro_rows, width), jnp.bfloat16)
    saved_inputs = blank
    tops = blank
    saved_mixed = jnp.zeros((MICRO, micro_rows, width), jnp.float32)
    received = jnp.zeros((micro_rows, width), jnp.bfloat16)
    forward_offset = jnp.where(spec_section, 0, section_index)
    takes_bag = spec_section | (section_index == 0)
    for moment in range(MICRO + top_section):
        micro_index = moment - forward_offset
        in_range = (micro_index >= 0) & (micro_index < MICRO)
        clipped = jnp.clip(micro_index, 0, MICRO - 1)
        from_bag = lax.dynamic_index_in_dim(first_inputs, clipped, 0, keepdims=False)
        current = jnp.where(takes_bag, from_bag, received)
        saved_inputs = keep_where(saved_inputs, current, clipped, in_range)
        output, mixed = layer_forward(current, layer_weights, gain)
        tops = keep_where(tops, output, clipped, in_range)
        saved_mixed = keep_where(saved_mixed, mixed, clipped, in_range)
        senders = [s for s in range(top_section) if 0 <= moment - s < MICRO]
        if senders == [top_section - 1]:
            received = hop(output, top_section - 1, top_section, last_section)
        elif senders:
            received = shift_pairs("section", [(s, s + 1) for s in senders])(output)
    proj = jnp.where(spec_section, spec_proj, prog_proj)
    unit, inverse, key = embed_rows(tops.reshape(sample_rows, width), proj)
    swap = shift_pairs("section", [(top_section, last_section), (last_section, top_section)])
    partner_key = swap(key)
    others = gather_rows(partner_key, "blk")
    scores = logit_scale * lax.dot_general(
        key, others, (((1,), (1,)), ((), ())), preferred_element_type=jnp.float32
    )
    row_max = jnp.max(scores, axis=1, keepdims=True)
    lse = row_max + jnp.log(jnp.sum(jnp.exp(scores - row_max), axis=1, keepdims=True))
    lse_down = shift_pairs("section", [(last_section, top_section)])(lse)
    lse_all = gather_rows(lse_down, "blk").reshape(1, -1)
    shift = jnp.where(spec_section, lse, lse_all)
    probs = jnp.exp(scores - shift).astype(jnp.bfloat16)
    dkey = logit_scale * (
        jnp.dot(probs, others, preferred_element_type=jnp.float32)
        - partner_key.astype(jnp.float32)
    )
    top_grad = embed_back(dkey, unit, inverse, proj).reshape(MICRO, micro_rows, width)
    saved_scaled = blank
    saved_dmixed = blank
    starts_grad = section_index >= top_section
    backward_offset = jnp.where(starts_grad, 0, top_section - section_index)
    incoming = jnp.zeros((micro_rows, width), jnp.bfloat16)
    for moment in range(MICRO + top_section):
        done = moment - 1
        senders = [s for s in range(1, top_section + 1) if 0 <= done - (top_section - s) < MICRO]
        if senders == [top_section]:
            incoming = hop(dhidden, top_section, top_section - 1, last_section)
        elif senders:
            incoming = shift_pairs("section", [(s, s - 1) for s in senders])(dhidden)
        micro_index = moment - backward_offset
        in_range = (micro_index >= 0) & (micro_index < MICRO)
        clipped = jnp.clip(micro_index, 0, MICRO - 1)
        upstream = jnp.where(
            starts_grad, lax.dynamic_index_in_dim(top_grad, clipped, 0, keepdims=False), incoming
        )
        hidden = lax.dynamic_index_in_dim(saved_inputs, clipped, 0, keepdims=False)
        mixed = lax.dynamic_index_in_dim(saved_mixed, clipped, 0, keepdims=False)
        dhidden, scaled, dmixed = layer_backward(hidden, upstream, layer_weights, gain, mixed)
        saved_scaled = keep_where(saved_scaled, scaled, clipped, in_range)
        saved_dmixed = keep_where(saved_dmixed, dmixed, clipped, in_range)
    scaled_all = saved_scaled.reshape(sample_rows, width)
    dmixed_all = saved_dmixed.reshape(sample_rows, width)
    partial = lax.dot_general(
        scaled_all, dmixed_all, (((0,), (0,)), ((), ())), preferred_element_type=jnp.float32
    )
    count = lax.axis_size("blk")
    pieces = partial.astype(jnp.bfloat16).reshape(count, width // count, width)
    landed = lax.all_to_all(pieces, "blk", 0, 0, tiled=True)
    return jnp.sum(landed.astype(jnp.float32), axis=0)


def solution(mesh):
    return jax.shard_map(
        local,
        mesh=mesh,
        in_specs=(
            P("blk", None),
            P("blk", None),
            P(),
            P(),
            P("section", None),
            P("section", None),
            P(),
            P(),
        ),
        out_specs=P(("section", "blk"), None),
        check_vma=False,
    )
```

```python
import jax
import jax.numpy as jnp
from jax import lax
from jax.sharding import PartitionSpec as P

L = 256
MICRO = 1
DIGIT = 32


logit_scale = 30.0
norm_eps = 1e-06


def shift_pairs(axis, pairs):
    return lambda value: lax.ppermute(value, axis, pairs)


def gather_rows(value, axis):
    count = lax.axis_size(axis)
    spread = jnp.broadcast_to(value[None], (count,) + value.shape)
    got = lax.all_to_all(spread, axis, 0, 0, tiled=True)
    return got.reshape((count * value.shape[0],) + value.shape[1:])


def layer_parts(hidden, weight, gain):
    wide = hidden.astype(jnp.float32)
    inverse = lax.rsqrt(jnp.mean(wide * wide, axis=1, keepdims=True) + norm_eps)
    normed = wide * inverse
    scaled = (normed * gain).astype(jnp.bfloat16)
    mixed = jnp.dot(scaled, weight, preferred_element_type=jnp.float32)
    return (wide, inverse, normed, scaled, mixed)


def layer_forward(hidden, weight, gain):
    wide, inverse, normed, scaled, mixed = layer_parts(hidden, weight, gain)
    return ((wide + mixed * jax.nn.sigmoid(mixed)).astype(jnp.bfloat16), mixed)


def layer_backward(hidden, upstream, weight, gain, mixed):
    wide = hidden.astype(jnp.float32)
    inverse = lax.rsqrt(jnp.mean(wide * wide, axis=1, keepdims=True) + norm_eps)
    normed = wide * inverse
    scaled = (normed * gain).astype(jnp.bfloat16)
    sigma = jax.nn.sigmoid(mixed)
    up_wide = upstream.astype(jnp.float32)
    dmixed = (up_wide * sigma * (1.0 + mixed * (1.0 - sigma))).astype(jnp.bfloat16)
    dnormed = (
        lax.dot_general(
            dmixed, weight, (((1,), (1,)), ((), ())), preferred_element_type=jnp.float32
        )
        * gain
    )
    dhidden = (
        up_wide + inverse * (dnormed - normed * jnp.mean(dnormed * normed, axis=1, keepdims=True))
    ).astype(jnp.bfloat16)
    return (dhidden, scaled, dmixed)


def embed_rows(hidden, proj):
    emb = jnp.dot(hidden, proj, preferred_element_type=jnp.float32)
    inverse = lax.rsqrt(jnp.sum(emb * emb, axis=1, keepdims=True) + norm_eps)
    unit = emb * inverse
    return (unit, inverse, unit.astype(jnp.bfloat16))


def embed_back(dkey, unit, inverse, proj):
    demb = (inverse * (dkey - unit * jnp.sum(unit * dkey, axis=1, keepdims=True))).astype(
        jnp.bfloat16
    )
    return lax.dot_general(
        demb, proj, (((1,), (1,)), ((), ())), preferred_element_type=jnp.float32
    ).astype(jnp.bfloat16)


def keep_where(buffer, value, index, valid):
    previous = lax.dynamic_index_in_dim(buffer, index, 0, keepdims=False)
    return lax.dynamic_update_index_in_dim(buffer, jnp.where(valid, value, previous), index, 0)


def local(prog_ids, spec_ids, prog_table, spec_table, layer_weights, gains, prog_proj, spec_proj):
    section_index = lax.axis_index("section")
    last_section = lax.axis_size("section") - 1
    top_section = last_section - 1
    spec_section = section_index == last_section
    token_ids = jnp.where(spec_section, spec_ids, prog_ids)
    table = jnp.where(spec_section, spec_table, prog_table)
    vocab = table.shape[0]
    high = (token_ids // DIGIT)[:, :, None] == jnp.arange(vocab // DIGIT, dtype=jnp.int32)
    low = (token_ids % DIGIT)[:, :, None] == jnp.arange(DIGIT, dtype=jnp.int32)
    counts = jnp.einsum(
        "bth,btl->bhl",
        high.astype(jnp.bfloat16),
        low.astype(jnp.bfloat16),
        preferred_element_type=jnp.float32,
    ).reshape(token_ids.shape[0], vocab).astype(jnp.bfloat16)
    sample_rows = prog_ids.shape[0]
    micro_rows = sample_rows // MICRO
    width = layer_weights.shape[1]
    first_inputs = (jnp.dot(counts, table, preferred_element_type=jnp.float32) * (1.0 / L)).astype(
        jnp.bfloat16
    )
    first_inputs = first_inputs.reshape(MICRO, micro_rows, width)
    gain = gains[0]
    blank = jnp.zeros((MICRO, micro_rows, width), jnp.bfloat16)
    saved_inputs = blank
    tops = blank
    mixed_steps = []
    received = jnp.zeros((micro_rows, width), jnp.bfloat16)
    forward_offset = jnp.where(spec_section, 0, section_index)
    takes_bag = spec_section | (section_index == 0)
    for moment in range(MICRO + top_section):
        micro_index = moment - forward_offset
        in_range = (micro_index >= 0) & (micro_index < MICRO)
        clipped = jnp.clip(micro_index, 0, MICRO - 1)
        from_bag = lax.dynamic_index_in_dim(first_inputs, clipped, 0, keepdims=False)
        current = jnp.where(takes_bag, from_bag, received)
        saved_inputs = keep_where(saved_inputs, current, clipped, in_range)
        output, mixed = layer_forward(current, layer_weights, gain)
        tops = keep_where(tops, output, clipped, in_range)
        mixed_steps.append((in_range, clipped, mixed))
        senders = [s for s in range(top_section) if 0 <= moment - s < MICRO]
        if senders:
            received = shift_pairs("section", [(s, s + 1) for s in senders])(output)
    proj = jnp.where(spec_section, spec_proj, prog_proj)
    unit, inverse, key = embed_rows(tops.reshape(sample_rows, width), proj)
    swap = shift_pairs("section", [(top_section, last_section), (last_section, top_section)])
    partner_key = swap(key)
    others = gather_rows(partner_key, "blk")
    scores = logit_scale * lax.dot_general(
        key, others, (((1,), (1,)), ((), ())), preferred_element_type=jnp.float32
    )
    row_max = jnp.max(scores, axis=1, keepdims=True)
    lse = row_max + jnp.log(jnp.sum(jnp.exp(scores - row_max), axis=1, keepdims=True))
    lse_down = shift_pairs("section", [(last_section, top_section)])(lse)
    lse_all = gather_rows(lse_down, "blk").reshape(1, -1)
    shift = jnp.where(spec_section, lse, lse_all)
    probs = jnp.exp(scores - shift).astype(jnp.bfloat16)
    dkey = logit_scale * (
        jnp.dot(probs, others, preferred_element_type=jnp.float32)
        - partner_key.astype(jnp.float32)
    )
    top_grad = embed_back(dkey, unit, inverse, proj).reshape(MICRO, micro_rows, width)
    saved_scaled = blank
    saved_dmixed = blank
    starts_grad = section_index >= top_section
    backward_offset = jnp.where(starts_grad, 0, top_section - section_index)
    incoming = jnp.zeros((micro_rows, width), jnp.bfloat16)
    for moment in range(MICRO + top_section):
        done = moment - 1
        senders = [s for s in range(1, top_section + 1) if 0 <= done - (top_section - s) < MICRO]
        if senders:
            incoming = shift_pairs("section", [(s, s - 1) for s in senders])(dhidden)
        micro_index = moment - backward_offset
        in_range = (micro_index >= 0) & (micro_index < MICRO)
        clipped = jnp.clip(micro_index, 0, MICRO - 1)
        upstream = jnp.where(
            starts_grad, lax.dynamic_index_in_dim(top_grad, clipped, 0, keepdims=False), incoming
        )
        hidden = lax.dynamic_index_in_dim(saved_inputs, clipped, 0, keepdims=False)
        mixed = jnp.zeros((micro_rows, width), jnp.float32)
        for kept, step_index, step_mixed in mixed_steps:
            mixed = jnp.where(kept & (step_index == clipped), step_mixed, mixed)
        dhidden, scaled, dmixed = layer_backward(hidden, upstream, layer_weights, gain, mixed)
        saved_scaled = keep_where(saved_scaled, scaled, clipped, in_range)
        saved_dmixed = keep_where(saved_dmixed, dmixed, clipped, in_range)
    scaled_all = saved_scaled.reshape(sample_rows, width)
    dmixed_all = saved_dmixed.reshape(sample_rows, width)
    partial = lax.dot_general(
        scaled_all, dmixed_all, (((0,), (0,)), ((), ())), preferred_element_type=jnp.float32
    )
    count = lax.axis_size("blk")
    pieces = partial.astype(jnp.bfloat16).reshape(count, width // count, width)
    landed = lax.all_to_all(pieces, "blk", 0, 0, tiled=True)
    return jnp.sum(landed.astype(jnp.float32), axis=0)


def solution(mesh):
    return jax.shard_map(
        local,
        mesh=mesh,
        in_specs=(
            P("blk", None),
            P("blk", None),
            P(),
            P(),
            P("section", None),
            P("section", None),
            P(),
            P(),
        ),
        out_specs=P(("section", "blk"), None),
        check_vma=False,
    )
```

```python
import jax
import jax.numpy as jnp
from jax import lax
from jax.sharding import PartitionSpec as P

L = 256
MICRO = 1
DIGIT = 32


logit_scale = 30.0
norm_eps = 1e-06


def shift_pairs(axis, pairs):
    return lambda value: lax.ppermute(value, axis, pairs)


def gather_rows(value, axis):
    count = lax.axis_size(axis)
    spread = jnp.broadcast_to(value[None], (count,) + value.shape)
    got = lax.all_to_all(spread, axis, 0, 0, tiled=True)
    return got.reshape((count * value.shape[0],) + value.shape[1:])


def layer_parts(hidden, weight, gain):
    wide = hidden.astype(jnp.float32)
    inverse = lax.rsqrt(jnp.mean(wide * wide, axis=1, keepdims=True) + norm_eps)
    normed = wide * inverse
    scaled = (normed * gain).astype(jnp.bfloat16)
    mixed = jnp.dot(scaled, weight, preferred_element_type=jnp.float32)
    return (wide, inverse, normed, scaled, mixed)


def layer_forward(hidden, weight, gain):
    wide, inverse, normed, scaled, mixed = layer_parts(hidden, weight, gain)
    return ((wide + mixed * jax.nn.sigmoid(mixed)).astype(jnp.bfloat16), mixed)


def layer_backward(hidden, upstream, weight, gain, mixed):
    wide = hidden.astype(jnp.float32)
    inverse = lax.rsqrt(jnp.mean(wide * wide, axis=1, keepdims=True) + norm_eps)
    normed = wide * inverse
    scaled = (normed * gain).astype(jnp.bfloat16)
    sigma = jax.nn.sigmoid(mixed)
    up_wide = upstream.astype(jnp.float32)
    dmixed = (up_wide * sigma * (1.0 + mixed * (1.0 - sigma))).astype(jnp.bfloat16)
    dnormed = (
        lax.dot_general(
            dmixed, weight, (((1,), (1,)), ((), ())), preferred_element_type=jnp.float32
        )
        * gain
    )
    dhidden = (
        up_wide + inverse * (dnormed - normed * jnp.mean(dnormed * normed, axis=1, keepdims=True))
    ).astype(jnp.bfloat16)
    return (dhidden, scaled, dmixed)


def embed_rows(hidden, proj):
    emb = jnp.dot(hidden, proj, preferred_element_type=jnp.float32)
    inverse = lax.rsqrt(jnp.sum(emb * emb, axis=1, keepdims=True) + norm_eps)
    unit = emb * inverse
    return (unit, inverse, unit.astype(jnp.bfloat16))


def embed_back(dkey, unit, inverse, proj):
    demb = (inverse * (dkey - unit * jnp.sum(unit * dkey, axis=1, keepdims=True))).astype(
        jnp.bfloat16
    )
    return lax.dot_general(
        demb, proj, (((1,), (1,)), ((), ())), preferred_element_type=jnp.float32
    ).astype(jnp.bfloat16)


def keep_where(buffer, value, index, valid):
    previous = lax.dynamic_index_in_dim(buffer, index, 0, keepdims=False)
    return lax.dynamic_update_index_in_dim(buffer, jnp.where(valid, value, previous), index, 0)


def local(prog_ids, spec_ids, prog_table, spec_table, layer_weights, gains, prog_proj, spec_proj):
    section_index = lax.axis_index("section")
    last_section = lax.axis_size("section") - 1
    top_section = last_section - 1
    spec_section = section_index == last_section
    token_ids = jnp.where(spec_section, spec_ids, prog_ids)
    table = jnp.where(spec_section, spec_table, prog_table)
    vocab = table.shape[0]
    high = (token_ids // DIGIT)[:, :, None] == jnp.arange(vocab // DIGIT, dtype=jnp.int32)
    low = (token_ids % DIGIT)[:, :, None] == jnp.arange(DIGIT, dtype=jnp.int32)
    counts = jnp.einsum(
        "bth,btl->bhl",
        high.astype(jnp.bfloat16),
        low.astype(jnp.bfloat16),
        preferred_element_type=jnp.float32,
    ).reshape(token_ids.shape[0], vocab).astype(jnp.bfloat16)
    sample_rows = prog_ids.shape[0]
    micro_rows = sample_rows // MICRO
    width = layer_weights.shape[1]
    first_inputs = (jnp.dot(counts, table, preferred_element_type=jnp.float32) * (1.0 / L)).astype(
        jnp.bfloat16
    )
    first_inputs = first_inputs.reshape(MICRO, micro_rows, width)
    gain = gains[0]
    blank = jnp.zeros((MICRO, micro_rows, width), jnp.bfloat16)
    saved_inputs = blank
    tops = blank
    saved_mixed = jnp.zeros((MICRO, micro_rows, width), jnp.float32)
    received = jnp.zeros((micro_rows, width), jnp.bfloat16)
    forward_offset = jnp.where(spec_section, 0, section_index)
    takes_bag = spec_section | (section_index == 0)
    for moment in range(MICRO + top_section):
        micro_index = moment - forward_offset
        in_range = (micro_index >= 0) & (micro_index < MICRO)
        clipped = jnp.clip(micro_index, 0, MICRO - 1)
        from_bag = lax.dynamic_index_in_dim(first_inputs, clipped, 0, keepdims=False)
        current = jnp.where(takes_bag, from_bag, received)
        saved_inputs = keep_where(saved_inputs, current, clipped, in_range)
        output, mixed = layer_forward(current, layer_weights, gain)
        tops = keep_where(tops, output, clipped, in_range)
        saved_mixed = keep_where(saved_mixed, mixed, clipped, in_range)
        senders = [s for s in range(top_section) if 0 <= moment - s < MICRO]
        if senders:
            received = shift_pairs("section", [(s, s + 1) for s in senders])(output)
    proj = jnp.where(spec_section, spec_proj, prog_proj)
    unit, inverse, key = embed_rows(tops.reshape(sample_rows, width), proj)
    swap = shift_pairs("section", [(top_section, last_section), (last_section, top_section)])
    partner_key = swap(key)
    others = gather_rows(partner_key, "blk")
    scores = logit_scale * lax.dot_general(
        key, others, (((1,), (1,)), ((), ())), preferred_element_type=jnp.float32
    )
    row_max = jnp.max(scores, axis=1, keepdims=True)
    lse = row_max + jnp.log(jnp.sum(jnp.exp(scores - row_max), axis=1, keepdims=True))
    lse_down = shift_pairs("section", [(last_section, top_section)])(lse)
    lse_down, unit, inverse = lax.optimization_barrier((lse_down, unit, inverse))
    lse_all = gather_rows(lse_down, "blk").reshape(1, -1)
    shift = jnp.where(spec_section, lse, lse_all)
    probs = jnp.exp(scores - shift).astype(jnp.bfloat16)
    dkey = logit_scale * (
        jnp.dot(probs, others, preferred_element_type=jnp.float32)
        - partner_key.astype(jnp.float32)
    )
    top_grad = embed_back(dkey, unit, inverse, proj).reshape(MICRO, micro_rows, width)
    saved_scaled = blank
    saved_dmixed = blank
    starts_grad = section_index >= top_section
    backward_offset = jnp.where(starts_grad, 0, top_section - section_index)
    incoming = jnp.zeros((micro_rows, width), jnp.bfloat16)
    for moment in range(MICRO + top_section):
        done = moment - 1
        senders = [s for s in range(1, top_section + 1) if 0 <= done - (top_section - s) < MICRO]
        if senders:
            incoming = shift_pairs("section", [(s, s - 1) for s in senders])(dhidden)
        micro_index = moment - backward_offset
        in_range = (micro_index >= 0) & (micro_index < MICRO)
        clipped = jnp.clip(micro_index, 0, MICRO - 1)
        upstream = jnp.where(
            starts_grad, lax.dynamic_index_in_dim(top_grad, clipped, 0, keepdims=False), incoming
        )
        hidden = lax.dynamic_index_in_dim(saved_inputs, clipped, 0, keepdims=False)
        mixed = lax.dynamic_index_in_dim(saved_mixed, clipped, 0, keepdims=False)
        dhidden, scaled, dmixed = layer_backward(hidden, upstream, layer_weights, gain, mixed)
        saved_scaled = keep_where(saved_scaled, scaled, clipped, in_range)
        saved_dmixed = keep_where(saved_dmixed, dmixed, clipped, in_range)
    scaled_all = saved_scaled.reshape(sample_rows, width)
    dmixed_all = saved_dmixed.reshape(sample_rows, width)
    partial = lax.dot_general(
        scaled_all, dmixed_all, (((0,), (0,)), ((), ())), preferred_element_type=jnp.float32
    )
    count = lax.axis_size("blk")
    pieces = partial.astype(jnp.bfloat16).reshape(count, width // count, width)
    landed = lax.all_to_all(pieces, "blk", 0, 0, tiled=True)
    return jnp.sum(landed.astype(jnp.float32), axis=0)


def solution(mesh):
    return jax.shard_map(
        local,
        mesh=mesh,
        in_specs=(
            P("blk", None),
            P("blk", None),
            P(),
            P(),
            P("section", None),
            P("section", None),
            P(),
            P(),
        ),
        out_specs=P(("section", "blk"), None),
        check_vma=False,
    )
```

```python
import jax
import jax.numpy as jnp
from jax import lax
from jax.sharding import PartitionSpec as P

L = 256
MICRO = 1
DIGIT = 32


logit_scale = 30.0
norm_eps = 1e-06


def shift_pairs(axis, pairs):
    return lambda value: lax.ppermute(value, axis, pairs)


def gather_rows(value, axis):
    count = lax.axis_size(axis)
    spread = jnp.broadcast_to(value[None], (count,) + value.shape)
    got = lax.all_to_all(spread, axis, 0, 0, tiled=True)
    return got.reshape((count * value.shape[0],) + value.shape[1:])


def layer_parts(hidden, weight, gain):
    wide = hidden.astype(jnp.float32)
    inverse = lax.rsqrt(jnp.mean(wide * wide, axis=1, keepdims=True) + norm_eps)
    normed = wide * inverse
    scaled = (normed * gain).astype(jnp.bfloat16)
    mixed = jnp.dot(scaled, weight, preferred_element_type=jnp.float32)
    return (wide, inverse, normed, scaled, mixed)


def layer_forward(hidden, weight, gain):
    wide, inverse, normed, scaled, mixed = layer_parts(hidden, weight, gain)
    return ((wide + mixed * jax.nn.sigmoid(mixed)).astype(jnp.bfloat16), mixed)


def layer_backward(hidden, upstream, weight, gain, mixed):
    wide = hidden.astype(jnp.float32)
    inverse = lax.rsqrt(jnp.mean(wide * wide, axis=1, keepdims=True) + norm_eps)
    normed = wide * inverse
    scaled = (normed * gain).astype(jnp.bfloat16)
    sigma = jax.nn.sigmoid(mixed)
    up_wide = upstream.astype(jnp.float32)
    dmixed = (up_wide * sigma * (1.0 + mixed * (1.0 - sigma))).astype(jnp.bfloat16)
    dnormed = (
        lax.dot_general(
            dmixed, weight, (((1,), (1,)), ((), ())), preferred_element_type=jnp.float32
        )
        * gain
    )
    dhidden = (
        up_wide + inverse * (dnormed - normed * jnp.mean(dnormed * normed, axis=1, keepdims=True))
    ).astype(jnp.bfloat16)
    return (dhidden, scaled, dmixed)


def embed_rows(hidden, proj):
    emb = jnp.dot(hidden, proj, preferred_element_type=jnp.float32)
    inverse = lax.rsqrt(jnp.sum(emb * emb, axis=1, keepdims=True) + norm_eps)
    unit = emb * inverse
    return (unit, inverse, unit.astype(jnp.bfloat16))


def embed_back(dkey, unit, inverse, proj):
    demb = (inverse * (dkey - unit * jnp.sum(unit * dkey, axis=1, keepdims=True))).astype(
        jnp.bfloat16
    )
    return lax.dot_general(
        demb, proj, (((1,), (1,)), ((), ())), preferred_element_type=jnp.float32
    ).astype(jnp.bfloat16)


def keep_where(buffer, value, index, valid):
    previous = lax.dynamic_index_in_dim(buffer, index, 0, keepdims=False)
    return lax.dynamic_update_index_in_dim(buffer, jnp.where(valid, value, previous), index, 0)


def local(prog_ids, spec_ids, prog_table, spec_table, layer_weights, gains, prog_proj, spec_proj):
    section_index = lax.axis_index("section")
    last_section = lax.axis_size("section") - 1
    top_section = last_section - 1
    spec_section = section_index == last_section
    token_ids, table = lax.cond(
        spec_section,
        lambda: (spec_ids, spec_table),
        lambda: (prog_ids, prog_table),
    )
    vocab = table.shape[0]
    high = (token_ids // DIGIT)[:, :, None] == jnp.arange(vocab // DIGIT, dtype=jnp.int32)
    low = (token_ids % DIGIT)[:, :, None] == jnp.arange(DIGIT, dtype=jnp.int32)
    counts = jnp.einsum(
        "bth,btl->bhl",
        high.astype(jnp.bfloat16),
        low.astype(jnp.bfloat16),
        preferred_element_type=jnp.float32,
    ).reshape(token_ids.shape[0], vocab).astype(jnp.bfloat16)
    sample_rows = prog_ids.shape[0]
    micro_rows = sample_rows // MICRO
    width = layer_weights.shape[1]
    first_inputs = (jnp.dot(counts, table, preferred_element_type=jnp.float32) * (1.0 / L)).astype(
        jnp.bfloat16
    )
    first_inputs = first_inputs.reshape(MICRO, micro_rows, width)
    gain = gains[0]
    blank = jnp.zeros((MICRO, micro_rows, width), jnp.bfloat16)
    saved_inputs = blank
    tops = blank
    saved_mixed = jnp.zeros((MICRO, micro_rows, width), jnp.float32)
    received = jnp.zeros((micro_rows, width), jnp.bfloat16)
    forward_offset = jnp.where(spec_section, 0, section_index)
    takes_bag = spec_section | (section_index == 0)
    for moment in range(MICRO + top_section):
        micro_index = moment - forward_offset
        in_range = (micro_index >= 0) & (micro_index < MICRO)
        clipped = jnp.clip(micro_index, 0, MICRO - 1)
        from_bag = lax.dynamic_index_in_dim(first_inputs, clipped, 0, keepdims=False)
        current = jnp.where(takes_bag, from_bag, received)
        saved_inputs = keep_where(saved_inputs, current, clipped, in_range)
        output, mixed = layer_forward(current, layer_weights, gain)
        tops = keep_where(tops, output, clipped, in_range)
        saved_mixed = keep_where(saved_mixed, mixed, clipped, in_range)
        senders = [s for s in range(top_section) if 0 <= moment - s < MICRO]
        if senders:
            received = shift_pairs("section", [(s, s + 1) for s in senders])(output)
    proj = jnp.where(spec_section, spec_proj, prog_proj)
    unit, inverse, key = embed_rows(tops.reshape(sample_rows, width), proj)
    swap = shift_pairs("section", [(top_section, last_section), (last_section, top_section)])
    partner_key = swap(key)
    others = gather_rows(partner_key, "blk")
    scores = logit_scale * lax.dot_general(
        key, others, (((1,), (1,)), ((), ())), preferred_element_type=jnp.float32
    )
    row_max = jnp.max(scores, axis=1, keepdims=True)
    lse = row_max + jnp.log(jnp.sum(jnp.exp(scores - row_max), axis=1, keepdims=True))
    lse_down = shift_pairs("section", [(last_section, top_section)])(lse)
    lse_all = gather_rows(lse_down, "blk").reshape(1, -1)
    shift = jnp.where(spec_section, lse, lse_all)
    probs = jnp.exp(scores - shift).astype(jnp.bfloat16)
    dkey = logit_scale * (
        jnp.dot(probs, others, preferred_element_type=jnp.float32)
        - partner_key.astype(jnp.float32)
    )
    top_grad = embed_back(dkey, unit, inverse, proj).reshape(MICRO, micro_rows, width)
    saved_scaled = blank
    saved_dmixed = blank
    starts_grad = section_index >= top_section
    backward_offset = jnp.where(starts_grad, 0, top_section - section_index)
    incoming = jnp.zeros((micro_rows, width), jnp.bfloat16)
    for moment in range(MICRO + top_section):
        done = moment - 1
        senders = [s for s in range(1, top_section + 1) if 0 <= done - (top_section - s) < MICRO]
        if senders:
            incoming = shift_pairs("section", [(s, s - 1) for s in senders])(dhidden)
        micro_index = moment - backward_offset
        in_range = (micro_index >= 0) & (micro_index < MICRO)
        clipped = jnp.clip(micro_index, 0, MICRO - 1)
        upstream = jnp.where(
            starts_grad, lax.dynamic_index_in_dim(top_grad, clipped, 0, keepdims=False), incoming
        )
        hidden = lax.dynamic_index_in_dim(saved_inputs, clipped, 0, keepdims=False)
        mixed = lax.dynamic_index_in_dim(saved_mixed, clipped, 0, keepdims=False)
        dhidden, scaled, dmixed = layer_backward(hidden, upstream, layer_weights, gain, mixed)
        saved_scaled = keep_where(saved_scaled, scaled, clipped, in_range)
        saved_dmixed = keep_where(saved_dmixed, dmixed, clipped, in_range)
    scaled_all = saved_scaled.reshape(sample_rows, width)
    dmixed_all = saved_dmixed.reshape(sample_rows, width)
    partial = lax.dot_general(
        scaled_all, dmixed_all, (((0,), (0,)), ((), ())), preferred_element_type=jnp.float32
    )
    count = lax.axis_size("blk")
    pieces = partial.astype(jnp.bfloat16).reshape(count, width // count, width)
    landed = lax.all_to_all(pieces, "blk", 0, 0, tiled=True)
    return jnp.sum(landed.astype(jnp.float32), axis=0)


def solution(mesh):
    return jax.shard_map(
        local,
        mesh=mesh,
        in_specs=(
            P("blk", None),
            P("blk", None),
            P(),
            P(),
            P("section", None),
            P("section", None),
            P(),
            P(),
        ),
        out_specs=P(("section", "blk"), None),
        check_vma=False,
    )
```

```python
import jax
import jax.numpy as jnp
from jax import lax
from jax.sharding import PartitionSpec as P

L = 256
MICRO = 1
DIGIT = 32


logit_scale = 30.0
norm_eps = 1e-06


def shift_pairs(axis, pairs):
    return lambda value: lax.ppermute(value, axis, pairs)


def gather_rows(value, axis):
    count = lax.axis_size(axis)
    spread = jnp.broadcast_to(value[None], (count,) + value.shape)
    got = lax.all_to_all(spread, axis, 0, 0, tiled=True)
    return got.reshape((count * value.shape[0],) + value.shape[1:])


def layer_parts(hidden, weight, gain):
    wide = hidden.astype(jnp.float32)
    inverse = lax.rsqrt(jnp.mean(wide * wide, axis=1, keepdims=True) + norm_eps)
    normed = wide * inverse
    scaled = (normed * gain).astype(jnp.bfloat16)
    mixed = jnp.dot(scaled, weight, preferred_element_type=jnp.float32)
    return (wide, inverse, normed, scaled, mixed)


def layer_forward(hidden, weight, gain):
    wide, inverse, normed, scaled, mixed = layer_parts(hidden, weight, gain)
    return ((wide + mixed * jax.nn.sigmoid(mixed)).astype(jnp.bfloat16), mixed)


def layer_backward(hidden, upstream, weight, gain, mixed):
    wide = hidden.astype(jnp.float32)
    inverse = lax.rsqrt(jnp.mean(wide * wide, axis=1, keepdims=True) + norm_eps)
    normed = wide * inverse
    scaled = (normed * gain).astype(jnp.bfloat16)
    sigma = jax.nn.sigmoid(mixed)
    up_wide = upstream.astype(jnp.float32)
    dmixed = (up_wide * sigma * (1.0 + mixed * (1.0 - sigma))).astype(jnp.bfloat16)
    dnormed = (
        lax.dot_general(
            dmixed, weight, (((1,), (1,)), ((), ())), preferred_element_type=jnp.float32
        )
        * gain
    )
    dhidden = (
        up_wide + inverse * (dnormed - normed * jnp.mean(dnormed * normed, axis=1, keepdims=True))
    ).astype(jnp.bfloat16)
    return (dhidden, scaled, dmixed)


def embed_rows(hidden, proj):
    emb = jnp.dot(hidden, proj, preferred_element_type=jnp.float32)
    inverse = lax.rsqrt(jnp.sum(emb * emb, axis=1, keepdims=True) + norm_eps)
    unit = emb * inverse
    return (unit, inverse, unit.astype(jnp.bfloat16))


def embed_back(dkey, unit, inverse, proj):
    demb = (inverse * (dkey - unit * jnp.sum(unit * dkey, axis=1, keepdims=True))).astype(
        jnp.bfloat16
    )
    return lax.dot_general(
        demb, proj, (((1,), (1,)), ((), ())), preferred_element_type=jnp.float32
    ).astype(jnp.bfloat16)


def keep_where(buffer, value, index, valid):
    previous = lax.dynamic_index_in_dim(buffer, index, 0, keepdims=False)
    return lax.dynamic_update_index_in_dim(buffer, jnp.where(valid, value, previous), index, 0)


def local(prog_ids, spec_ids, prog_table, spec_table, layer_weights, gains, prog_proj, spec_proj):
    section_index = lax.axis_index("section")
    last_section = lax.axis_size("section") - 1
    top_section = last_section - 1
    spec_section = section_index == last_section
    token_ids, table = lax.cond(
        spec_section,
        lambda: (spec_ids, spec_table),
        lambda: (prog_ids, prog_table),
    )
    vocab = table.shape[0]
    high = (token_ids // DIGIT)[:, :, None] == jnp.arange(vocab // DIGIT, dtype=jnp.int32)
    low = (token_ids % DIGIT)[:, :, None] == jnp.arange(DIGIT, dtype=jnp.int32)
    counts = jnp.einsum(
        "bth,btl->bhl",
        high.astype(jnp.bfloat16),
        low.astype(jnp.bfloat16),
        preferred_element_type=jnp.float32,
    ).reshape(token_ids.shape[0], vocab).astype(jnp.bfloat16)
    sample_rows = prog_ids.shape[0]
    micro_rows = sample_rows // MICRO
    width = layer_weights.shape[1]
    first_inputs = (jnp.dot(counts, table, preferred_element_type=jnp.float32) * (1.0 / L)).astype(
        jnp.bfloat16
    )
    first_inputs = first_inputs.reshape(MICRO, micro_rows, width)
    gain = gains[0]
    blank = jnp.zeros((MICRO, micro_rows, width), jnp.bfloat16)
    saved_inputs = blank
    tops = blank
    saved_mixed = jnp.zeros((MICRO, micro_rows, width), jnp.float32)
    received = jnp.zeros((micro_rows, width), jnp.bfloat16)
    forward_offset = jnp.where(spec_section, 0, section_index)
    takes_bag = spec_section | (section_index == 0)
    for moment in range(MICRO + top_section):
        micro_index = moment - forward_offset
        in_range = (micro_index >= 0) & (micro_index < MICRO)
        clipped = jnp.clip(micro_index, 0, MICRO - 1)
        from_bag = lax.dynamic_index_in_dim(first_inputs, clipped, 0, keepdims=False)
        current = jnp.where(takes_bag, from_bag, received)
        saved_inputs = keep_where(saved_inputs, current, clipped, in_range)
        output, mixed = layer_forward(current, layer_weights, gain)
        tops = keep_where(tops, output, clipped, in_range)
        saved_mixed = keep_where(saved_mixed, mixed, clipped, in_range)
        senders = [s for s in range(top_section) if 0 <= moment - s < MICRO]
        if senders:
            received = shift_pairs("section", [(s, s + 1) for s in senders])(output)
    proj = lax.cond(spec_section, lambda: spec_proj, lambda: prog_proj)
    unit, inverse, key = embed_rows(tops.reshape(sample_rows, width), proj)
    swap = shift_pairs("section", [(top_section, last_section), (last_section, top_section)])
    partner_key = swap(key)
    others = gather_rows(partner_key, "blk")
    scores = logit_scale * lax.dot_general(
        key, others, (((1,), (1,)), ((), ())), preferred_element_type=jnp.float32
    )
    row_max = jnp.max(scores, axis=1, keepdims=True)
    lse = row_max + jnp.log(jnp.sum(jnp.exp(scores - row_max), axis=1, keepdims=True))
    lse_down = shift_pairs("section", [(last_section, top_section)])(lse)
    lse_all = gather_rows(lse_down, "blk").reshape(1, -1)
    shift = jnp.where(spec_section, lse, lse_all)
    probs = jnp.exp(scores - shift).astype(jnp.bfloat16)
    dkey = logit_scale * (
        jnp.dot(probs, others, preferred_element_type=jnp.float32)
        - partner_key.astype(jnp.float32)
    )
    top_grad = embed_back(dkey, unit, inverse, proj).reshape(MICRO, micro_rows, width)
    saved_scaled = blank
    saved_dmixed = blank
    starts_grad = section_index >= top_section
    backward_offset = jnp.where(starts_grad, 0, top_section - section_index)
    incoming = jnp.zeros((micro_rows, width), jnp.bfloat16)
    for moment in range(MICRO + top_section):
        done = moment - 1
        senders = [s for s in range(1, top_section + 1) if 0 <= done - (top_section - s) < MICRO]
        if senders:
            incoming = shift_pairs("section", [(s, s - 1) for s in senders])(dhidden)
        micro_index = moment - backward_offset
        in_range = (micro_index >= 0) & (micro_index < MICRO)
        clipped = jnp.clip(micro_index, 0, MICRO - 1)
        upstream = jnp.where(
            starts_grad, lax.dynamic_index_in_dim(top_grad, clipped, 0, keepdims=False), incoming
        )
        hidden = lax.dynamic_index_in_dim(saved_inputs, clipped, 0, keepdims=False)
        mixed = lax.dynamic_index_in_dim(saved_mixed, clipped, 0, keepdims=False)
        dhidden, scaled, dmixed = layer_backward(hidden, upstream, layer_weights, gain, mixed)
        saved_scaled = keep_where(saved_scaled, scaled, clipped, in_range)
        saved_dmixed = keep_where(saved_dmixed, dmixed, clipped, in_range)
    scaled_all = saved_scaled.reshape(sample_rows, width)
    dmixed_all = saved_dmixed.reshape(sample_rows, width)
    partial = lax.dot_general(
        scaled_all, dmixed_all, (((0,), (0,)), ((), ())), preferred_element_type=jnp.float32
    )
    count = lax.axis_size("blk")
    pieces = partial.astype(jnp.bfloat16).reshape(count, width // count, width)
    landed = lax.all_to_all(pieces, "blk", 0, 0, tiled=True)
    return jnp.sum(landed.astype(jnp.float32), axis=0)


def solution(mesh):
    return jax.shard_map(
        local,
        mesh=mesh,
        in_specs=(
            P("blk", None),
            P("blk", None),
            P(),
            P(),
            P("section", None),
            P("section", None),
            P(),
            P(),
        ),
        out_specs=P(("section", "blk"), None),
        check_vma=False,
    )
```

```python
import jax
import jax.numpy as jnp
from jax import lax
from jax.sharding import PartitionSpec as P

L = 256
MICRO = 1
DIGIT = 16


logit_scale = 30.0
norm_eps = 1e-06


def shift_pairs(axis, pairs):
    return lambda value: lax.ppermute(value, axis, pairs)


def gather_rows(value, axis):
    count = lax.axis_size(axis)
    spread = jnp.broadcast_to(value[None], (count,) + value.shape)
    got = lax.all_to_all(spread, axis, 0, 0, tiled=True)
    return got.reshape((count * value.shape[0],) + value.shape[1:])


def layer_parts(hidden, weight, gain):
    wide = hidden.astype(jnp.float32)
    inverse = lax.rsqrt(jnp.mean(wide * wide, axis=1, keepdims=True) + norm_eps)
    normed = wide * inverse
    scaled = (normed * gain).astype(jnp.bfloat16)
    mixed = jnp.dot(scaled, weight, preferred_element_type=jnp.float32)
    return (wide, inverse, normed, scaled, mixed)


def layer_forward(hidden, weight, gain):
    wide, inverse, normed, scaled, mixed = layer_parts(hidden, weight, gain)
    return ((wide + mixed * jax.nn.sigmoid(mixed)).astype(jnp.bfloat16), mixed)


def layer_backward(hidden, upstream, weight, gain, mixed):
    wide = hidden.astype(jnp.float32)
    inverse = lax.rsqrt(jnp.mean(wide * wide, axis=1, keepdims=True) + norm_eps)
    normed = wide * inverse
    scaled = (normed * gain).astype(jnp.bfloat16)
    sigma = jax.nn.sigmoid(mixed)
    up_wide = upstream.astype(jnp.float32)
    dmixed = (up_wide * sigma * (1.0 + mixed * (1.0 - sigma))).astype(jnp.bfloat16)
    dnormed = (
        lax.dot_general(
            dmixed, weight, (((1,), (1,)), ((), ())), preferred_element_type=jnp.float32
        )
        * gain
    )
    dhidden = (
        up_wide + inverse * (dnormed - normed * jnp.mean(dnormed * normed, axis=1, keepdims=True))
    ).astype(jnp.bfloat16)
    return (dhidden, scaled, dmixed)


def embed_rows(hidden, proj):
    emb = jnp.dot(hidden, proj, preferred_element_type=jnp.float32)
    inverse = lax.rsqrt(jnp.sum(emb * emb, axis=1, keepdims=True) + norm_eps)
    unit = emb * inverse
    return (unit, inverse, unit.astype(jnp.bfloat16))


def embed_back(dkey, unit, inverse, proj):
    demb = (inverse * (dkey - unit * jnp.sum(unit * dkey, axis=1, keepdims=True))).astype(
        jnp.bfloat16
    )
    return lax.dot_general(
        demb, proj, (((1,), (1,)), ((), ())), preferred_element_type=jnp.float32
    ).astype(jnp.bfloat16)


def keep_where(buffer, value, index, valid):
    previous = lax.dynamic_index_in_dim(buffer, index, 0, keepdims=False)
    return lax.dynamic_update_index_in_dim(buffer, jnp.where(valid, value, previous), index, 0)


def local(prog_ids, spec_ids, prog_table, spec_table, layer_weights, gains, prog_proj, spec_proj):
    section_index = lax.axis_index("section")
    last_section = lax.axis_size("section") - 1
    top_section = last_section - 1
    spec_section = section_index == last_section
    token_ids, table = lax.cond(
        spec_section,
        lambda: (spec_ids, spec_table),
        lambda: (prog_ids, prog_table),
    )
    vocab = table.shape[0]
    high = (token_ids // DIGIT)[:, :, None] == jnp.arange(vocab // DIGIT, dtype=jnp.int32)
    low = (token_ids % DIGIT)[:, :, None] == jnp.arange(DIGIT, dtype=jnp.int32)
    counts = jnp.einsum(
        "bth,btl->bhl",
        high.astype(jnp.bfloat16),
        low.astype(jnp.bfloat16),
        preferred_element_type=jnp.float32,
    ).reshape(token_ids.shape[0], vocab).astype(jnp.bfloat16)
    sample_rows = prog_ids.shape[0]
    micro_rows = sample_rows // MICRO
    width = layer_weights.shape[1]
    first_inputs = (jnp.dot(counts, table, preferred_element_type=jnp.float32) * (1.0 / L)).astype(
        jnp.bfloat16
    )
    first_inputs = first_inputs.reshape(MICRO, micro_rows, width)
    gain = gains[0]
    blank = jnp.zeros((MICRO, micro_rows, width), jnp.bfloat16)
    saved_inputs = blank
    tops = blank
    saved_mixed = jnp.zeros((MICRO, micro_rows, width), jnp.float32)
    received = jnp.zeros((micro_rows, width), jnp.bfloat16)
    forward_offset = jnp.where(spec_section, 0, section_index)
    takes_bag = spec_section | (section_index == 0)
    for moment in range(MICRO + top_section):
        micro_index = moment - forward_offset
        in_range = (micro_index >= 0) & (micro_index < MICRO)
        clipped = jnp.clip(micro_index, 0, MICRO - 1)
        from_bag = lax.dynamic_index_in_dim(first_inputs, clipped, 0, keepdims=False)
        current = jnp.where(takes_bag, from_bag, received)
        saved_inputs = keep_where(saved_inputs, current, clipped, in_range)
        output, mixed = layer_forward(current, layer_weights, gain)
        tops = keep_where(tops, output, clipped, in_range)
        saved_mixed = keep_where(saved_mixed, mixed, clipped, in_range)
        senders = [s for s in range(top_section) if 0 <= moment - s < MICRO]
        if senders:
            received = shift_pairs("section", [(s, s + 1) for s in senders])(output)
    proj = jnp.where(spec_section, spec_proj, prog_proj)
    unit, inverse, key = embed_rows(tops.reshape(sample_rows, width), proj)
    swap = shift_pairs("section", [(top_section, last_section), (last_section, top_section)])
    partner_key = swap(key)
    others = gather_rows(partner_key, "blk")
    scores = logit_scale * lax.dot_general(
        key, others, (((1,), (1,)), ((), ())), preferred_element_type=jnp.float32
    )
    row_max = jnp.max(scores, axis=1, keepdims=True)
    lse = row_max + jnp.log(jnp.sum(jnp.exp(scores - row_max), axis=1, keepdims=True))
    lse_down = shift_pairs("section", [(last_section, top_section)])(lse)
    lse_all = gather_rows(lse_down, "blk").reshape(1, -1)
    shift = jnp.where(spec_section, lse, lse_all)
    probs = jnp.exp(scores - shift).astype(jnp.bfloat16)
    dkey = logit_scale * (
        jnp.dot(probs, others, preferred_element_type=jnp.float32)
        - partner_key.astype(jnp.float32)
    )
    top_grad = embed_back(dkey, unit, inverse, proj).reshape(MICRO, micro_rows, width)
    saved_scaled = blank
    saved_dmixed = blank
    starts_grad = section_index >= top_section
    backward_offset = jnp.where(starts_grad, 0, top_section - section_index)
    incoming = jnp.zeros((micro_rows, width), jnp.bfloat16)
    for moment in range(MICRO + top_section):
        done = moment - 1
        senders = [s for s in range(1, top_section + 1) if 0 <= done - (top_section - s) < MICRO]
        if senders:
            incoming = shift_pairs("section", [(s, s - 1) for s in senders])(dhidden)
        micro_index = moment - backward_offset
        in_range = (micro_index >= 0) & (micro_index < MICRO)
        clipped = jnp.clip(micro_index, 0, MICRO - 1)
        upstream = jnp.where(
            starts_grad, lax.dynamic_index_in_dim(top_grad, clipped, 0, keepdims=False), incoming
        )
        hidden = lax.dynamic_index_in_dim(saved_inputs, clipped, 0, keepdims=False)
        mixed = lax.dynamic_index_in_dim(saved_mixed, clipped, 0, keepdims=False)
        dhidden, scaled, dmixed = layer_backward(hidden, upstream, layer_weights, gain, mixed)
        saved_scaled = keep_where(saved_scaled, scaled, clipped, in_range)
        saved_dmixed = keep_where(saved_dmixed, dmixed, clipped, in_range)
    scaled_all = saved_scaled.reshape(sample_rows, width)
    dmixed_all = saved_dmixed.reshape(sample_rows, width)
    partial = lax.dot_general(
        scaled_all, dmixed_all, (((0,), (0,)), ((), ())), preferred_element_type=jnp.float32
    )
    count = lax.axis_size("blk")
    pieces = partial.astype(jnp.bfloat16).reshape(count, width // count, width)
    landed = lax.all_to_all(pieces, "blk", 0, 0, tiled=True)
    return jnp.sum(landed.astype(jnp.float32), axis=0)


def solution(mesh):
    return jax.shard_map(
        local,
        mesh=mesh,
        in_specs=(
            P("blk", None),
            P("blk", None),
            P(),
            P(),
            P("section", None),
            P("section", None),
            P(),
            P(),
        ),
        out_specs=P(("section", "blk"), None),
        check_vma=False,
    )
```
